32 devices in a mesh: req: 16 (over z, y, x), head: 2 (over core).
Axes of the slice: x: 2, y: 2, z: 4, core: 2. Of those that a mesh axis runs over, the one named last changes fastest.
Arguments:
- hidden: bfloat16 [384, 1024], P('req', 'head'), may hold values from -6 to 6
- norm_gain: float32 [1024], replicated, may hold values from 0.1 to 1.9
- qkv_weight: bfloat16 [1024, 8, 3, 128], P(None, 'head'), may hold values from -0.1875 to 0.1875
- conv_weight: float32 [4, 8, 3, 128], P(None, 'head'), may hold values from -1.5 to 1.5
- conv_state: bfloat16 [384, 3, 8, 3, 128], P('req', None, 'head'), may hold values from -6 to 6
- gate_weight: bfloat16 [1024, 2, 8], P(None, None, 'head'), may hold values from -0.1875 to 0.1875
- prompt_weight: float32 [384, 8], P('req', 'head'), may hold values from 0.2 to 1
- ridge_term: float32 [8], P('head'), may hold values from 0.25 to 1
- own_keys: float32 [384, 8, 128, 128], P('req', 'head'), as said below
- own_values: float32 [384, 8, 128, 128], P('req', 'head')
- prompt_keys: float32 [32, 8, 128, 128], P('req', 'head'), as said below
- prompt_values: float32 [32, 8, 128, 128], P('req', 'head')
- group_ids: int32 [384], P('req'), may hold values from 0 to 31, as said below
- lengths: int32 [384], P('req'), may hold values from 0 to 32768, as said below
- out_weight: bfloat16 [8, 128, 1024], P('head'), may hold values from -0.1875 to 0.1875
Outputs:
- combined: bfloat16 [384, 1024], P('req', 'head')
The draws below stay inside these ranges and needn't reach their ends.
Inputs may be any that keep to these rules, and one draw needn't show every extreme that they name: `group_ids`: group g's prompt states are row g of prompt_keys and prompt_values. Every group holds 8 to 16 request slots, some group exactly 8 and some exactly 16. The groups held by one index of req hold exactly 24 slots in all. The slots of one index of req form runs of 6 consecutive slots; the groups of one run are all held by one index of req, and different runs of one index by different indices. So at most 6 live requests of one index of req belong to groups held by one index of req, and some pair of indices reaches it. `lengths`: 0 marks an empty slot. At most half of the slots of one index of req are empty; some index has none empty and some exactly half. Some live requests hold 1 token and some 2. `own_keys`: each [128, 128] matrix is symmetric positive semidefinite. `prompt_keys`: each [128, 128] matrix is symmetric positive semidefinite.
All inputs are finite; a program needn't handle non-finite values.
Results may differ from the reference program's by a relative error of at most 0.008.
Values may be sent and summed in bfloat16 or wider, within the bound.
No kernel may reach another device: no remote copies, remote signals or barrier semaphores. Data moves between devices by JAX's collectives and lax.ppermute only.
A program may use at most 128 MiB of HBM per device.

```python
import math
import jax
import jax.numpy as jnp
from jax import lax

D = 1024
H = 8
DH = 128
KW = 4
ITERS = 8
MAXLEN = 32768
REQUEST_SLOTS = 24
GROUPS = 32
REQUESTS = 384
N_REQ = 16


def gram_states(base_key, matrix_count, columns):

    def single(subkey):
        key_basis, key_values = jax.random.split(subkey, 2)
        basis_cols = jax.random.normal(key_basis, (H, DH, columns), jnp.float32)
        values = jax.random.normal(key_values, (H, DH, columns), jnp.float32)
        keys_state = jnp.einsum('hic,hjc->hij', basis_cols, basis_cols, precision=lax.Precision.HIGHEST) / columns
        keys_state = 0.5 * (keys_state + jnp.swapaxes(keys_state, 1, 2))
        values_state = jnp.einsum('hic,hjc->hij', values, basis_cols, precision=lax.Precision.HIGHEST) / columns
        return (keys_state, values_state)
    return lax.map(single, jax.random.split(base_key, matrix_count))


def draw_own_keys(key, part):
    return gram_states(jax.random.fold_in(key, 7), REQUESTS, DH)[0]


def draw_own_values(key, part):
    return gram_states(jax.random.fold_in(key, 7), REQUESTS, DH)[1]


def draw_prompt_keys(key, part):
    return gram_states(jax.random.fold_in(key, 13), GROUPS, 2 * DH)[0]


def draw_prompt_values(key, part):
    return gram_states(jax.random.fold_in(key, 13), GROUPS, 2 * DH)[1]


def draw_group_ids(key, part):
    replica_count = REQUESTS // REQUEST_SLOTS
    groups_here = REQUEST_SLOTS // 12
    run_length = REQUEST_SLOTS // 4
    subkeys = jax.random.split(key, 5)
    shuffle_a = jax.random.permutation(subkeys[0], replica_count)
    shuffle_b = jax.random.permutation(subkeys[1], replica_count)
    offsets = jax.random.permutation(subkeys[2], replica_count)
    position_all = jnp.arange(REQUESTS)
    device_of = position_all // REQUEST_SLOTS
    slot_of = position_all % REQUEST_SLOTS
    owner_of = shuffle_b[(shuffle_a[device_of] + offsets[slot_of // run_length]) % replica_count]
    scores = jax.random.randint(subkeys[3], (replica_count, REQUEST_SLOTS), 0, 2 ** 20) * REQUEST_SLOTS + jnp.arange(REQUEST_SLOTS)[None, :]
    placement = jnp.argsort(jnp.argsort(scores, axis=1), axis=1)
    shifts = jax.random.randint(subkeys[4], (replica_count, groups_here // 2), -4, 5)
    shifts = shifts.at[0, 0].set(4)
    group_sizes = jnp.stack([12 + shifts, 12 - shifts], axis=2).reshape(replica_count, groups_here)
    bounds = jnp.cumsum(group_sizes, axis=1)
    arrival = placement[owner_of, slot_of]
    within = jnp.sum((arrival[:, None] >= bounds[owner_of]).astype(jnp.int32), axis=1)
    return (owner_of * groups_here + within).astype(jnp.int32)


def draw_lengths(key, part):
    replica_count = REQUESTS // REQUEST_SLOTS
    empty_key_mask, key_order, key_sizes, key_short = jax.random.split(key, 4)
    empty_slots = jax.random.randint(empty_key_mask, (replica_count,), 0, REQUEST_SLOTS // 2 + 1)
    empty_slots = empty_slots.at[0].set(0).at[1].set(REQUEST_SLOTS // 2)
    scores = jax.random.randint(key_order, (replica_count, REQUEST_SLOTS), 0, 2 ** 20) * REQUEST_SLOTS + jnp.arange(REQUEST_SLOTS)[None, :]
    rank_order = jnp.argsort(jnp.argsort(scores, axis=1), axis=1)
    context = jax.random.randint(key_sizes, (replica_count, REQUEST_SLOTS), 1, MAXLEN + 1)
    chosen = (jax.random.randint(key_short, (replica_count,), 0, 3) == 0) | (jnp.arange(replica_count) == 1)
    context = jnp.where(chosen[:, None] & (rank_order == REQUEST_SLOTS - 1), 1, context)
    context = jnp.where(chosen[:, None] & (rank_order == REQUEST_SLOTS - 2), 2, context)
    context = context.at[0, 0].set(MAXLEN)
    mask_of_live = rank_order >= empty_slots[:, None]
    return jnp.where(mask_of_live, context, 0).reshape(REQUESTS).astype(jnp.int32)


def block_levels(stream_key, shape, cuts, least, high):
    loudness, own = 1.0, jax.random.fold_in(stream_key, 6)
    for position, parts in cuts:
        draws = jnp.exp(jax.random.uniform(jax.random.fold_in(own, position), (parts,), jnp.float32, least / len(cuts), high / len(cuts)))
        loudness = loudness * jnp.repeat(draws, shape[position] // parts).reshape([-1 if axis == position else 1 for axis in range(len(shape))])
    return loudness


def scatter_about(rng, shape, deviation, reach, cuts=(), kind=jnp.bfloat16):
    factor_of = block_levels(rng, shape, cuts, -0.22, 0.18) if cuts else 1.0
    drawn = jax.random.normal(rng, shape, jnp.float32) * deviation * factor_of
    return jnp.minimum(jnp.maximum(drawn, -reach), reach).astype(kind)


def setup_inputs(seed: int = 0) -> dict:
    key_of = jax.random.split(jax.random.key(seed), 16)
    hidden = scatter_about(key_of[0], (REQUESTS, D), 1.0, 6.0, ((0, 16), (1, 2)))
    norm_gain = jnp.clip(1.0 + 0.18 * jax.random.normal(key_of[1], (D,), jnp.float32), 0.1, 1.9)
    qkv_weight = scatter_about(key_of[2], (D, H, 3, DH), D ** -0.5, 0.1875, ((1, 2),))
    conv_weight = scatter_about(key_of[3], (KW, H, 3, DH), 0.5, 1.5, ((1, 2),), jnp.float32)
    conv_state = scatter_about(key_of[4], (REQUESTS, KW - 1, H, 3, DH), 1.0, 6.0, ((0, 16), (2, 2)))
    gate_weight = scatter_about(key_of[5], (D, 2, H), D ** -0.5, 0.1875, ((2, 2),))
    prompt_weight = jnp.clip(jnp.exp(math.log(1.0) - 1.609438 * jax.random.uniform(key_of[6], (REQUESTS, H), jnp.float32) ** block_levels(key_of[6], (REQUESTS, H), ((0, 16), (1, 2)), -0.2, 0.2)), 0.2, 1.0)
    ridge_term = jnp.clip(jnp.exp(math.log(1.0) - 1.3862944 * jax.random.uniform(key_of[7], (H,), jnp.float32) ** block_levels(key_of[7], (H,), ((0, 2),), -0.2, 0.2)), 0.25, 1.0)
    own_keys = draw_own_keys(jax.random.fold_in(key_of[15], 71), 0)
    own_values = draw_own_values(jax.random.fold_in(key_of[15], 71), 0)
    prompt_keys = draw_prompt_keys(jax.random.fold_in(key_of[15], 71), 0)
    prompt_values = draw_prompt_values(jax.random.fold_in(key_of[15], 71), 0)
    group_ids = draw_group_ids(jax.random.fold_in(key_of[15], 71), 0)
    lengths = draw_lengths(jax.random.fold_in(key_of[15], 71), 0)
    out_weight = scatter_about(key_of[14], (H, DH, D), (H * DH) ** -0.5, 0.1875, ((0, 2),))
    return {"hidden": hidden, "norm_gain": norm_gain, "qkv_weight": qkv_weight, "conv_weight": conv_weight, "conv_state": conv_state, "gate_weight": gate_weight, "prompt_weight": prompt_weight, "ridge_term": ridge_term, "own_keys": own_keys, "own_values": own_values, "prompt_keys": prompt_keys, "prompt_values": prompt_values, "group_ids": group_ids, "lengths": lengths, "out_weight": out_weight}


epsilon = 1e-06
highest = lax.Precision.HIGHEST

def matvec(matrices, vectors):
    return jnp.einsum('bhij,bhj->bhi', matrices, vectors, precision=highest)

def reference(hidden, norm_gain, qkv_weight, conv_weight, conv_state, gate_weight, prompt_weight, ridge_term, own_keys, own_values, prompt_keys, prompt_values, group_ids, lengths, out_weight):
    widened = hidden.astype(jnp.float32)
    scaled = widened * lax.rsqrt(lax.optimization_barrier(jnp.mean(widened * widened, axis=1, keepdims=True)) + epsilon) * norm_gain
    normed = scaled.astype(jnp.bfloat16)
    projected = jnp.dot(normed, qkv_weight.reshape(D, H * 3 * DH), preferred_element_type=jnp.float32).reshape(REQUESTS, H, 3, DH)
    mixing = conv_weight[0] * projected
    for offset in range(1, KW):
        usable = (lengths >= offset).astype(jnp.float32)[:, None, None, None]
        mixing = mixing + conv_weight[offset] * conv_state[:, offset - 1].astype(jnp.float32) * usable
    active = jax.nn.silu(mixing)
    queries = active[:, :, 0]
    queries = queries * lax.rsqrt(lax.optimization_barrier(jnp.sum(queries * queries, axis=2, keepdims=True)) + epsilon)
    key_now = active[:, :, 1]
    key_now = key_now * lax.rsqrt(lax.optimization_barrier(jnp.sum(key_now * key_now, axis=2, keepdims=True)) + epsilon)
    value_now = active[:, :, 2]
    gate_logit = jnp.dot(normed, gate_weight.reshape(D, 2 * H), preferred_element_type=jnp.float32).reshape(REQUESTS, 2, H)
    decay_rate = jax.nn.sigmoid(gate_logit[:, 0])
    write_rate = jax.nn.sigmoid(gate_logit[:, 1])

    def blocked(array):
        return array.reshape((N_REQ, REQUEST_SLOTS) + array.shape[1:])

    def solve_block(pieces):
        block_queries, block_keys, block_values, block_decay, block_write, weight_of_block, state_keys, state_values, block_groups = pieces
        keys_per_group = prompt_keys[block_groups]
        group_values = prompt_values[block_groups]
        decay_col = block_decay[:, :, None]
        write_col = block_write[:, :, None]
        weight_col = weight_of_block[:, :, None]
        ridge_col = ridge_term[None, :, None]

        def operator_apply(direction):
            shared = weight_col * matvec(keys_per_group, direction) + matvec(state_keys, direction)
            return decay_col * shared + write_col * block_keys * lax.optimization_barrier(jnp.sum(block_keys * direction, axis=2, keepdims=True)) + ridge_col * direction
        solution = jnp.zeros_like(block_queries)
        residual = block_queries
        direction = block_queries
        norm_now = lax.optimization_barrier(jnp.sum(residual * residual, axis=2, keepdims=True))
        for iteration in range(ITERS):
            product = operator_apply(direction)
            step_size = norm_now / lax.optimization_barrier(jnp.sum(direction * product, axis=2, keepdims=True))
            solution = solution + step_size * direction
            residual = residual - step_size * product
            norm_next = lax.optimization_barrier(jnp.sum(residual * residual, axis=2, keepdims=True))
            direction = residual + norm_next / norm_now * direction
            norm_now = norm_next
        shared_out = weight_col * matvec(group_values, solution) + matvec(state_values, solution)
        return decay_col * shared_out + write_col * block_values * lax.optimization_barrier(jnp.sum(block_keys * solution, axis=2, keepdims=True))
    readout = lax.map(solve_block, (blocked(queries), blocked(key_now), blocked(value_now), blocked(decay_rate), blocked(write_rate), blocked(prompt_weight), blocked(own_keys), blocked(own_values), blocked(group_ids)))
    readout = readout.reshape(REQUESTS, H, DH)
    normalized = (readout * lax.rsqrt(lax.optimization_barrier(jnp.mean(readout * readout, axis=2, keepdims=True)) + epsilon)).astype(jnp.bfloat16)
    attended = jnp.dot(normalized.reshape(REQUESTS, H * DH), out_weight.reshape(H * DH, D), preferred_element_type=jnp.float32)
    live_column = (lengths > 0).astype(jnp.float32)[:, None]
    return (widened + live_column * attended).astype(jnp.bfloat16)
```

```python
import jax
import jax.numpy as jnp
from jax import lax
from jax.sharding import PartitionSpec as P

KW = 4
ITERS = 8
CAP = 6


epsilon = 1e-06
highest = lax.Precision.HIGHEST


def own_matvec(matrices, vectors):
    return jnp.sum(matrices * vectors[:, :, None, :], axis=3)


def on_device(
    hidden,
    norm_gain,
    qkv_weight,
    conv_weight,
    conv_state,
    gate_weight,
    prompt_weight,
    ridge_term,
    own_keys,
    own_values,
    prompt_keys,
    prompt_values,
    group_ids,
    lengths,
    out_weight,
):
    gathered = lax.all_gather(hidden, "head", axis=1, tiled=True)
    widened = gathered.astype(jnp.float32)
    scaled = (
        widened
        * lax.rsqrt(jnp.mean(widened * widened, axis=1, keepdims=True) + epsilon)
        * norm_gain
    )
    normed = scaled.astype(jnp.bfloat16)
    row_count, model_width = gathered.shape
    head_count = qkv_weight.shape[1]
    head_size = qkv_weight.shape[3]
    projected = jnp.dot(
        normed,
        qkv_weight.reshape(model_width, head_count * 3 * head_size),
        preferred_element_type=jnp.float32,
    ).reshape(row_count, head_count, 3, head_size)
    mixing = conv_weight[0] * projected
    for offset in range(1, KW):
        usable = (lengths >= offset).astype(jnp.float32)[:, None, None, None]
        mixing = (
            mixing + conv_weight[offset] * conv_state[:, offset - 1].astype(jnp.float32) * usable
        )
    active = jax.nn.silu(mixing)
    queries = active[:, :, 0]
    queries = queries * lax.rsqrt(jnp.sum(queries * queries, axis=2, keepdims=True) + epsilon)
    key_now = active[:, :, 1]
    key_now = key_now * lax.rsqrt(jnp.sum(key_now * key_now, axis=2, keepdims=True) + epsilon)
    value_now = active[:, :, 2]
    gate_logit = jnp.dot(
        normed, gate_weight.reshape(model_width, 2 * head_count), preferred_element_type=jnp.float32
    ).reshape(row_count, 2, head_count)
    decay_col = jax.nn.sigmoid(gate_logit[:, 0])[:, :, None]
    write_col = jax.nn.sigmoid(gate_logit[:, 1])[:, :, None]
    weight_col = prompt_weight[:, :, None]
    ridge_col = ridge_term[None, :, None]

    peer_count = lax.axis_size("req")
    group_count = prompt_keys.shape[0]
    capacity = CAP
    slot_count = peer_count * capacity
    mask_of_live = lengths > 0
    owner_of = group_ids // group_count
    local_group = group_ids % group_count
    order_ids = jnp.arange(row_count)
    earlier = (
        (order_ids[None, :] < order_ids[:, None])
        & (owner_of[None, :] == owner_of[:, None])
        & mask_of_live[None, :]
    )
    rank_of = jnp.sum(earlier.astype(jnp.int32), axis=1)
    routed = mask_of_live & (rank_of < capacity)
    slot_of = jnp.where(routed, owner_of * capacity + rank_of, 0)
    hits = (slot_of[:, None] == jnp.arange(slot_count)[None, :]) & routed[:, None]
    filled = jnp.any(hits, axis=0)
    source = jnp.sum(jnp.where(hits, order_ids[:, None], 0), axis=0) + jnp.where(
        filled, 0, row_count
    )
    slot_label = jnp.sum(jnp.where(hits, (local_group + 1)[:, None], 0), axis=0)

    def pack(vectors):
        padded = jnp.concatenate(
            [vectors, jnp.zeros((1,) + vectors.shape[1:], vectors.dtype)], axis=0
        )
        return jnp.take(padded, source, axis=0)

    def exchange(slots):
        shaped = slots.reshape((peer_count, capacity) + slots.shape[1:])
        moved = lax.all_to_all(shaped, "req", split_axis=0, concat_axis=0, tiled=True)
        return moved.reshape(slots.shape)

    def unpack(slots):
        taken = jnp.take(slots, slot_of, axis=0)
        return jnp.where(routed[:, None, None], taken, 0.0)

    def owner_apply(states, incoming, chosen):
        products = jnp.einsum("shj,ghij->gshi", incoming, states, precision=highest)
        total = jnp.zeros_like(incoming)
        for group in range(group_count):
            total = total + jnp.where(chosen[group][:, None, None], products[group], 0.0)
        return total

    solution = jnp.zeros_like(queries)
    residual = queries
    direction = queries
    norm_now = jnp.sum(residual * residual, axis=2, keepdims=True)
    chosen = None
    for iteration in range(ITERS):
        outgoing = pack(direction)
        if iteration == 0:
            label_row = jnp.broadcast_to(
                slot_label.astype(jnp.float32)[:, None, None], (slot_count, 1, head_size)
            )
            arrived = exchange(jnp.concatenate([outgoing, label_row], axis=1))
            labels_in = arrived[:, head_count, 0]
            chosen = [labels_in == float(group + 1) for group in range(group_count)]
            arrived = arrived[:, :head_count]
        else:
            arrived = exchange(outgoing)
        shares = unpack(exchange(owner_apply(prompt_keys, arrived, chosen)))
        shared = weight_col * shares + own_matvec(own_keys, direction)
        product = (
            decay_col * shared
            + write_col * key_now * jnp.sum(key_now * direction, axis=2, keepdims=True)
            + ridge_col * direction
        )
        step_size = norm_now / jnp.sum(direction * product, axis=2, keepdims=True)
        solution = solution + step_size * direction
        residual = residual - step_size * product
        norm_next = jnp.sum(residual * residual, axis=2, keepdims=True)
        direction = residual + norm_next / norm_now * direction
        norm_now = norm_next
    value_sum = unpack(exchange(owner_apply(prompt_values, exchange(pack(solution)), chosen)))
    shared_out = weight_col * value_sum + own_matvec(own_values, solution)
    readout = decay_col * shared_out + write_col * value_now * jnp.sum(
        key_now * solution, axis=2, keepdims=True
    )
    normalized = (
        readout * lax.rsqrt(jnp.mean(readout * readout, axis=2, keepdims=True) + epsilon)
    ).astype(jnp.bfloat16)
    partial_value = jnp.dot(
        normalized.reshape(row_count, head_count * head_size),
        out_weight.reshape(head_count * head_size, model_width),
        preferred_element_type=jnp.float32,
    )
    head_peers = lax.axis_size("head")
    if head_peers == 2:
        me = lax.axis_index("head")
        width = model_width // 2
        mine = lax.dynamic_slice_in_dim(partial_value, me * width, width, axis=1)
        theirs = lax.dynamic_slice_in_dim(partial_value, (1 - me) * width, width, axis=1)
        attended = mine + lax.ppermute(theirs, "head", [(0, 1), (1, 0)])
    else:
        attended = lax.psum_scatter(
            partial_value.astype(jnp.bfloat16), "head", scatter_dimension=1, tiled=True
        ).astype(jnp.float32)
    widened_own = hidden.astype(jnp.float32)
    combined = jnp.where(mask_of_live[:, None], widened_own + attended, widened_own)
    return combined.astype(jnp.bfloat16)


def solution(mesh):
    in_specs = (
        P("req", "head"),
        P(),
        P(None, "head", None, None),
        P(None, "head", None, None),
        P("req", None, "head", None, None),
        P(None, None, "head"),
        P("req", "head"),
        P("head"),
        P("req", "head", None, None),
        P("req", "head", None, None),
        P("req", "head", None, None),
        P("req", "head", None, None),
        P("req"),
        P("req"),
        P("head", None, None),
    )
    out_specs = P("req", "head")
    return jax.shard_map(
        on_device, mesh=mesh, in_specs=in_specs, out_specs=out_specs, check_vma=False
    )
```

```python
import jax
import jax.numpy as jnp
from jax import lax
from jax.experimental import pallas as pl
from jax.experimental.pallas import tpu as pltpu
from jax.sharding import PartitionSpec as P

KW = 4
ITERS = 8
CAP = 6


epsilon = 1e-06
highest = lax.Precision.HIGHEST


def own_matvec(matrices, vectors):
    return jnp.sum(matrices * vectors[:, :, None, :], axis=3)


def project_kernel(rows_ref, weight_ref, out_ref):
    out_ref[...] = jnp.dot(rows_ref[...], weight_ref[...], preferred_element_type=jnp.float32)


def project(rows, weight):
    row_count, depth = rows.shape
    width = weight.shape[1]
    return pl.pallas_call(
        project_kernel,
        out_shape=jax.ShapeDtypeStruct((row_count, width), jnp.float32),
        in_specs=[pl.BlockSpec(memory_space=pltpu.VMEM)] * 2,
        out_specs=pl.BlockSpec(memory_space=pltpu.VMEM),
        cost_estimate=pl.CostEstimate(
            flops=2 * row_count * depth * width,
            bytes_accessed=2 * (row_count * depth + depth * width) + 4 * row_count * width,
            transcendentals=0,
        ),
    )(rows, weight)


def on_device(
    hidden,
    norm_gain,
    qkv_weight,
    conv_weight,
    conv_state,
    gate_weight,
    prompt_weight,
    ridge_term,
    own_keys,
    own_values,
    prompt_keys,
    prompt_values,
    group_ids,
    lengths,
    out_weight,
):
    gathered = lax.all_gather(hidden, "head", axis=1, tiled=True)
    widened = gathered.astype(jnp.float32)
    scaled = (
        widened
        * lax.rsqrt(jnp.mean(widened * widened, axis=1, keepdims=True) + epsilon)
        * norm_gain
    )
    normed = scaled.astype(jnp.bfloat16)
    row_count, model_width = gathered.shape
    head_count = qkv_weight.shape[1]
    head_size = qkv_weight.shape[3]
    projected = project(
        normed, qkv_weight.reshape(model_width, head_count * 3 * head_size)
    ).reshape(row_count, head_count, 3, head_size)
    mixing = conv_weight[0] * projected
    for offset in range(1, KW):
        usable = (lengths >= offset).astype(jnp.float32)[:, None, None, None]
        mixing = (
            mixing + conv_weight[offset] * conv_state[:, offset - 1].astype(jnp.float32) * usable
        )
    active = jax.nn.silu(mixing)
    queries = active[:, :, 0]
    queries = queries * lax.rsqrt(jnp.sum(queries * queries, axis=2, keepdims=True) + epsilon)
    key_now = active[:, :, 1]
    key_now = key_now * lax.rsqrt(jnp.sum(key_now * key_now, axis=2, keepdims=True) + epsilon)
    value_now = active[:, :, 2]
    gate_logit = jnp.dot(
        normed, gate_weight.reshape(model_width, 2 * head_count), preferred_element_type=jnp.float32
    ).reshape(row_count, 2, head_count)
    decay_col = jax.nn.sigmoid(gate_logit[:, 0])[:, :, None]
    write_col = jax.nn.sigmoid(gate_logit[:, 1])[:, :, None]
    weight_col = prompt_weight[:, :, None]
    ridge_col = ridge_term[None, :, None]

    peer_count = lax.axis_size("req")
    group_count = prompt_keys.shape[0]
    capacity = CAP
    slot_count = peer_count * capacity
    mask_of_live = lengths > 0
    owner_of = group_ids // group_count
    local_group = group_ids % group_count
    order_ids = jnp.arange(row_count)
    earlier = (
        (order_ids[None, :] < order_ids[:, None])
        & (owner_of[None, :] == owner_of[:, None])
        & mask_of_live[None, :]
    )
    rank_of = jnp.sum(earlier.astype(jnp.int32), axis=1)
    routed = mask_of_live & (rank_of < capacity)
    slot_of = jnp.where(routed, owner_of * capacity + rank_of, 0)
    hits = (slot_of[:, None] == jnp.arange(slot_count)[None, :]) & routed[:, None]
    filled = jnp.any(hits, axis=0)
    source = jnp.sum(jnp.where(hits, order_ids[:, None], 0), axis=0) + jnp.where(
        filled, 0, row_count
    )
    slot_label = jnp.sum(jnp.where(hits, (local_group + 1)[:, None], 0), axis=0)

    def pack(vectors):
        padded = jnp.concatenate(
            [vectors, jnp.zeros((1,) + vectors.shape[1:], vectors.dtype)], axis=0
        )
        return jnp.take(padded, source, axis=0)

    def exchange(slots):
        shaped = slots.reshape((peer_count, capacity) + slots.shape[1:])
        moved = lax.all_to_all(shaped, "req", split_axis=0, concat_axis=0, tiled=True)
        return moved.reshape(slots.shape)

    def unpack(slots):
        taken = jnp.take(slots, slot_of, axis=0)
        return jnp.where(routed[:, None, None], taken, 0.0)

    def owner_apply(states, incoming, chosen):
        split = jnp.stack(
            [jnp.where(chosen[group][:, None, None], incoming, 0.0) for group in range(group_count)]
        )
        return jnp.einsum("gshj,ghij->shi", split, states, precision=highest)

    def cg_step(arrived, carry):
        solution, residual, direction, norm_now = carry
        shares = unpack(exchange(owner_apply(prompt_keys, arrived, chosen)))
        shared = weight_col * shares + own_matvec(own_keys, direction)
        product = (
            decay_col * shared
            + write_col * key_now * jnp.sum(key_now * direction, axis=2, keepdims=True)
            + ridge_col * direction
        )
        step_size = norm_now / jnp.sum(direction * product, axis=2, keepdims=True)
        solution = solution + step_size * direction
        residual = residual - step_size * product
        norm_next = jnp.sum(residual * residual, axis=2, keepdims=True)
        direction = residual + norm_next / norm_now * direction
        return solution, residual, direction, norm_next

    label_row = jnp.broadcast_to(
        slot_label.astype(jnp.float32)[:, None, None], (slot_count, 1, head_size)
    )
    first = exchange(jnp.concatenate([pack(queries), label_row], axis=1))
    labels_in = first[:, head_count, 0]
    chosen = [labels_in == float(group + 1) for group in range(group_count)]
    carry = (
        jnp.zeros_like(queries),
        queries,
        queries,
        jnp.sum(queries * queries, axis=2, keepdims=True),
    )
    carry = cg_step(first[:, :head_count], carry)
    carry = lax.fori_loop(
        1, ITERS, lambda _, state: cg_step(exchange(pack(state[2])), state), carry
    )
    solution = carry[0]
    value_sum = unpack(exchange(owner_apply(prompt_values, exchange(pack(solution)), chosen)))
    shared_out = weight_col * value_sum + own_matvec(own_values, solution)
    readout = decay_col * shared_out + write_col * value_now * jnp.sum(
        key_now * solution, axis=2, keepdims=True
    )
    normalized = (
        readout * lax.rsqrt(jnp.mean(readout * readout, axis=2, keepdims=True) + epsilon)
    ).astype(jnp.bfloat16)
    partial_value = jnp.dot(
        normalized.reshape(row_count, head_count * head_size),
        out_weight.reshape(head_count * head_size, model_width),
        preferred_element_type=jnp.float32,
    )
    head_peers = lax.axis_size("head")
    if head_peers == 2:
        me = lax.axis_index("head")
        width = model_width // 2
        mine = lax.dynamic_slice_in_dim(partial_value, me * width, width, axis=1)
        theirs = lax.dynamic_slice_in_dim(partial_value, (1 - me) * width, width, axis=1)
        attended = mine + lax.ppermute(theirs, "head", [(0, 1), (1, 0)])
    else:
        attended = lax.psum_scatter(
            partial_value.astype(jnp.bfloat16), "head", scatter_dimension=1, tiled=True
        ).astype(jnp.float32)
    widened_own = hidden.astype(jnp.float32)
    combined = jnp.where(mask_of_live[:, None], widened_own + attended, widened_own)
    return combined.astype(jnp.bfloat16)


def solution(mesh):
    in_specs = (
        P("req", "head"),
        P(),
        P(None, "head", None, None),
        P(None, "head", None, None),
        P("req", None, "head", None, None),
        P(None, None, "head"),
        P("req", "head"),
        P("head"),
        P("req", "head", None, None),
        P("req", "head", None, None),
        P("req", "head", None, None),
        P("req", "head", None, None),
        P("req"),
        P("req"),
        P("head", None, None),
    )
    out_specs = P("req", "head")
    return jax.shard_map(
        on_device, mesh=mesh, in_specs=in_specs, out_specs=out_specs, check_vma=False
    )
```

```python
import jax
import jax.numpy as jnp
from jax import lax
from jax.sharding import PartitionSpec as P

KW = 4
ITERS = 8
CAP = 6


epsilon = 1e-06
highest = lax.Precision.HIGHEST


def own_matvec(matrices, vectors):
    return jnp.sum(matrices * vectors[:, :, None, :], axis=3)


def on_device(
    hidden,
    norm_gain,
    qkv_weight,
    conv_weight,
    conv_state,
    gate_weight,
    prompt_weight,
    ridge_term,
    own_keys,
    own_values,
    prompt_keys,
    prompt_values,
    group_ids,
    lengths,
    out_weight,
):
    gathered = lax.all_gather(hidden, "head", axis=1, tiled=True)
    widened = gathered.astype(jnp.float32)
    scaled = (
        widened
        * lax.rsqrt(jnp.mean(widened * widened, axis=1, keepdims=True) + epsilon)
        * norm_gain
    )
    normed = scaled.astype(jnp.bfloat16)
    row_count, model_width = gathered.shape
    head_count = qkv_weight.shape[1]
    head_size = qkv_weight.shape[3]
    projected = jnp.dot(
        normed,
        qkv_weight.reshape(model_width, head_count * 3 * head_size),
        preferred_element_type=jnp.float32,
    ).reshape(row_count, head_count, 3, head_size)
    mixing = conv_weight[0] * projected
    for offset in range(1, KW):
        usable = (lengths >= offset).astype(jnp.float32)[:, None, None, None]
        mixing = (
            mixing + conv_weight[offset] * conv_state[:, offset - 1].astype(jnp.float32) * usable
        )
    active = jax.nn.silu(mixing)
    queries = active[:, :, 0]
    queries = queries * lax.rsqrt(jnp.sum(queries * queries, axis=2, keepdims=True) + epsilon)
    key_now = active[:, :, 1]
    key_now = key_now * lax.rsqrt(jnp.sum(key_now * key_now, axis=2, keepdims=True) + epsilon)
    value_now = active[:, :, 2]
    gate_logit = jnp.dot(
        normed, gate_weight.reshape(model_width, 2 * head_count), preferred_element_type=jnp.float32
    ).reshape(row_count, 2, head_count)
    decay_col = jax.nn.sigmoid(gate_logit[:, 0])[:, :, None]
    write_col = jax.nn.sigmoid(gate_logit[:, 1])[:, :, None]
    weight_col = prompt_weight[:, :, None]
    ridge_col = ridge_term[None, :, None]

    peer_count = lax.axis_size("req")
    group_count = prompt_keys.shape[0]
    capacity = CAP
    slot_count = peer_count * capacity
    mask_of_live = lengths > 0
    owner_of = group_ids // group_count
    local_group = group_ids % group_count
    order_ids = jnp.arange(row_count)
    earlier = (
        (order_ids[None, :] < order_ids[:, None])
        & (owner_of[None, :] == owner_of[:, None])
        & mask_of_live[None, :]
    )
    rank_of = jnp.sum(earlier.astype(jnp.int32), axis=1)
    routed = mask_of_live & (rank_of < capacity)
    slot_of = jnp.where(routed, owner_of * capacity + rank_of, 0)
    hits = (slot_of[:, None] == jnp.arange(slot_count)[None, :]) & routed[:, None]
    filled = jnp.any(hits, axis=0)
    source = jnp.sum(jnp.where(hits, order_ids[:, None], 0), axis=0) + jnp.where(
        filled, 0, row_count
    )
    slot_label = jnp.sum(jnp.where(hits, (local_group + 1)[:, None], 0), axis=0)

    def pack(vectors):
        padded = jnp.concatenate(
            [vectors, jnp.zeros((1,) + vectors.shape[1:], vectors.dtype)], axis=0
        )
        return jnp.take(padded, source, axis=0)

    def exchange(slots):
        shaped = slots.astype(jnp.bfloat16).reshape((peer_count, capacity) + slots.shape[1:])
        moved = lax.all_to_all(shaped, "req", split_axis=0, concat_axis=0, tiled=True)
        return moved.reshape(slots.shape).astype(jnp.float32)

    def unpack(slots):
        taken = jnp.take(slots, slot_of, axis=0)
        return jnp.where(routed[:, None, None], taken, 0.0)

    def owner_apply(states, incoming, chosen):
        split = jnp.stack(
            [jnp.where(chosen[group][:, None, None], incoming, 0.0) for group in range(group_count)]
        )
        return jnp.einsum("gshj,ghij->shi", split, states, precision=highest)

    def cg_step(arrived, carry):
        solution, residual, direction, norm_now = carry
        shares = unpack(exchange(owner_apply(prompt_keys, arrived, chosen)))
        shared = weight_col * shares + own_matvec(own_keys, direction)
        product = (
            decay_col * shared
            + write_col * key_now * jnp.sum(key_now * direction, axis=2, keepdims=True)
            + ridge_col * direction
        )
        step_size = norm_now / jnp.sum(direction * product, axis=2, keepdims=True)
        solution = solution + step_size * direction
        residual = residual - step_size * product
        norm_next = jnp.sum(residual * residual, axis=2, keepdims=True)
        direction = residual + norm_next / norm_now * direction
        return solution, residual, direction, norm_next

    label_row = jnp.broadcast_to(
        slot_label.astype(jnp.float32)[:, None, None], (slot_count, 1, head_size)
    )
    first = exchange(jnp.concatenate([pack(queries), label_row], axis=1))
    labels_in = first[:, head_count, 0]
    chosen = [labels_in == float(group + 1) for group in range(group_count)]
    carry = (
        jnp.zeros_like(queries),
        queries,
        queries,
        jnp.sum(queries * queries, axis=2, keepdims=True),
    )
    carry = cg_step(first[:, :head_count], carry)
    carry = lax.fori_loop(
        1, ITERS, lambda _, state: cg_step(exchange(pack(state[2])), state), carry
    )
    solution = carry[0]
    value_sum = unpack(exchange(owner_apply(prompt_values, exchange(pack(solution)), chosen)))
    shared_out = weight_col * value_sum + own_matvec(own_values, solution)
    readout = decay_col * shared_out + write_col * value_now * jnp.sum(
        key_now * solution, axis=2, keepdims=True
    )
    normalized = (
        readout * lax.rsqrt(jnp.mean(readout * readout, axis=2, keepdims=True) + epsilon)
    ).astype(jnp.bfloat16)
    partial_value = jnp.dot(
        normalized.reshape(row_count, head_count * head_size),
        out_weight.reshape(head_count * head_size, model_width),
        preferred_element_type=jnp.float32,
    )
    head_peers = lax.axis_size("head")
    if head_peers == 2:
        me = lax.axis_index("head")
        width = model_width // 2
        mine = lax.dynamic_slice_in_dim(partial_value, me * width, width, axis=1)
        theirs = lax.dynamic_slice_in_dim(partial_value, (1 - me) * width, width, axis=1)
        attended = mine + lax.ppermute(theirs, "head", [(0, 1), (1, 0)])
    else:
        attended = lax.psum_scatter(
            partial_value.astype(jnp.bfloat16), "head", scatter_dimension=1, tiled=True
        ).astype(jnp.float32)
    widened_own = hidden.astype(jnp.float32)
    combined = jnp.where(mask_of_live[:, None], widened_own + attended, widened_own)
    return combined.astype(jnp.bfloat16)


def solution(mesh):
    in_specs = (
        P("req", "head"),
        P(),
        P(None, "head", None, None),
        P(None, "head", None, None),
        P("req", None, "head", None, None),
        P(None, None, "head"),
        P("req", "head"),
        P("head"),
        P("req", "head", None, None),
        P("req", "head", None, None),
        P("req", "head", None, None),
        P("req", "head", None, None),
        P("req"),
        P("req"),
        P("head", None, None),
    )
    out_specs = P("req", "head")
    return jax.shard_map(
        on_device, mesh=mesh, in_specs=in_specs, out_specs=out_specs, check_vma=False
    )
```

```python
import jax
import jax.numpy as jnp
from jax import lax
from jax.sharding import PartitionSpec as P

KW = 4
ITERS = 8
CAP = 6


epsilon = 1e-06
highest = lax.Precision.HIGHEST


def own_matvec(matrices, vectors):
    return jnp.sum(matrices * vectors[:, :, None, :], axis=3)


def on_device(
    hidden,
    norm_gain,
    qkv_weight,
    conv_weight,
    conv_state,
    gate_weight,
    prompt_weight,
    ridge_term,
    own_keys,
    own_values,
    prompt_keys,
    prompt_values,
    group_ids,
    lengths,
    out_weight,
):
    gathered = lax.all_gather(hidden, "head", axis=1, tiled=True)
    widened = gathered.astype(jnp.float32)
    scaled = (
        widened
        * lax.rsqrt(jnp.mean(widened * widened, axis=1, keepdims=True) + epsilon)
        * norm_gain
    )
    normed = scaled.astype(jnp.bfloat16)
    row_count, model_width = gathered.shape
    head_count = qkv_weight.shape[1]
    head_size = qkv_weight.shape[3]
    projected = jnp.dot(
        normed,
        qkv_weight.reshape(model_width, head_count * 3 * head_size),
        preferred_element_type=jnp.float32,
    ).reshape(row_count, head_count, 3, head_size)
    mixing = conv_weight[0] * projected
    for offset in range(1, KW):
        usable = (lengths >= offset).astype(jnp.float32)[:, None, None, None]
        mixing = (
            mixing + conv_weight[offset] * conv_state[:, offset - 1].astype(jnp.float32) * usable
        )
    active = jax.nn.silu(mixing)
    queries = active[:, :, 0]
    queries = queries * lax.rsqrt(jnp.sum(queries * queries, axis=2, keepdims=True) + epsilon)
    key_now = active[:, :, 1]
    key_now = key_now * lax.rsqrt(jnp.sum(key_now * key_now, axis=2, keepdims=True) + epsilon)
    value_now = active[:, :, 2]
    gate_logit = jnp.dot(
        normed, gate_weight.reshape(model_width, 2 * head_count), preferred_element_type=jnp.float32
    ).reshape(row_count, 2, head_count)
    decay_col = jax.nn.sigmoid(gate_logit[:, 0])[:, :, None]
    write_col = jax.nn.sigmoid(gate_logit[:, 1])[:, :, None]
    weight_col = prompt_weight[:, :, None]
    ridge_col = ridge_term[None, :, None]

    peer_count = lax.axis_size("req")
    group_count = prompt_keys.shape[0]
    capacity = CAP
    slot_count = peer_count * capacity
    mask_of_live = lengths > 0
    owner_of = group_ids // group_count
    local_group = group_ids % group_count
    order_ids = jnp.arange(row_count)
    earlier = (
        (order_ids[None, :] < order_ids[:, None])
        & (owner_of[None, :] == owner_of[:, None])
        & mask_of_live[None, :]
    )
    rank_of = jnp.sum(earlier.astype(jnp.int32), axis=1)
    routed = mask_of_live & (rank_of < capacity)
    slot_of = jnp.where(routed, owner_of * capacity + rank_of, 0)
    hits = (slot_of[:, None] == jnp.arange(slot_count)[None, :]) & routed[:, None]
    filled = jnp.any(hits, axis=0)
    source = jnp.sum(jnp.where(hits, order_ids[:, None], 0), axis=0) + jnp.where(
        filled, 0, row_count
    )
    slot_label = jnp.sum(jnp.where(hits, (local_group + 1)[:, None], 0), axis=0)

    def pack(vectors):
        padded = jnp.concatenate(
            [vectors, jnp.zeros((1,) + vectors.shape[1:], vectors.dtype)], axis=0
        )
        return jnp.take(padded, source, axis=0)

    def exchange(slots):
        shaped = slots.reshape((peer_count, capacity) + slots.shape[1:])
        moved = lax.all_to_all(shaped, "req", split_axis=0, concat_axis=0, tiled=True)
        return moved.reshape(slots.shape)

    def unpack(slots):
        taken = jnp.take(slots, slot_of, axis=0)
        return jnp.where(routed[:, None, None], taken, 0.0)

    def owner_apply(states, incoming, chosen):
        split = jnp.stack(
            [jnp.where(chosen[group][:, None, None], incoming, 0.0) for group in range(group_count)]
        )
        return jnp.einsum("gshj,ghij->shi", split, states, precision=highest)

    def lane_row(values):
        return jnp.pad(values, ((0, 0), (0, head_size - values.shape[1])))[:, None, :]

    def requester_step(shares, solution, residual, direction, norm_now):
        shared = weight_col * shares + own_matvec(own_keys, direction)
        product = (
            decay_col * shared
            + write_col * key_now * jnp.sum(key_now * direction, axis=2, keepdims=True)
            + ridge_col * direction
        )
        step_size = norm_now / jnp.sum(direction * product, axis=2, keepdims=True)
        solution = solution + step_size * direction
        residual = residual - step_size * product
        norm_next = jnp.sum(residual * residual, axis=2, keepdims=True)
        direction = residual + norm_next / norm_now * direction
        return solution, residual, direction, norm_next, step_size

    label_row = lane_row(slot_label.astype(jnp.float32)[:, None])
    first = exchange(jnp.concatenate([pack(queries), label_row], axis=1))
    labels_in = first[:, head_count, 0]
    chosen = [labels_in == float(group + 1) for group in range(group_count)]
    slot_used = labels_in > 0.5
    held = first[:, :head_count]
    shares = unpack(exchange(owner_apply(prompt_keys, held, chosen)))
    norm_first = jnp.sum(queries * queries, axis=2, keepdims=True)
    state = requester_step(shares, jnp.zeros_like(queries), queries, queries, norm_first)

    def middle_step(_, carry):
        solution, residual, direction, norm_now, step_prev, held, running = carry
        step_row = lane_row(pack(step_prev[:, :, 0]))
        arrived = exchange(jnp.concatenate([pack(direction), step_row], axis=1))
        running = running + arrived[:, head_count, :head_count][:, :, None] * held
        held = arrived[:, :head_count]
        shares = unpack(exchange(owner_apply(prompt_keys, held, chosen)))
        return requester_step(shares, solution, residual, direction, norm_now) + (held, running)

    carry = lax.fori_loop(1, ITERS - 1, middle_step, state + (held, jnp.zeros_like(held)))
    solution, residual, direction, norm_now, step_prev, held, running = carry

    local_part = (
        decay_col * own_matvec(own_keys, direction)
        + write_col * key_now * jnp.sum(key_now * direction, axis=2, keepdims=True)
        + ridge_col * direction
    )
    local_curve = jnp.sum(direction * local_part, axis=2)
    scalars = jnp.concatenate(
        [step_prev[:, :, 0], norm_now[:, :, 0], local_curve, (decay_col * weight_col)[:, :, 0]],
        axis=1,
    )
    arrived = exchange(jnp.concatenate([pack(direction), lane_row(pack(scalars))], axis=1))
    extra = arrived[:, head_count]
    running = running + extra[:, :head_count][:, :, None] * held
    held = arrived[:, :head_count]
    prompt_part = owner_apply(prompt_keys, held, chosen)
    prompt_curve = jnp.sum(held * prompt_part, axis=2)
    rr_in = extra[:, head_count : 2 * head_count]
    curve = extra[:, 2 * head_count : 3 * head_count] + extra[:, 3 * head_count : 4 * head_count] * prompt_curve
    step_last = jnp.where(slot_used[:, None], rr_in / jnp.where(slot_used[:, None], curve, 1.0), 0.0)
    running = running + step_last[:, :, None] * held
    finished = owner_apply(prompt_values, running, chosen)
    returned = unpack(exchange(jnp.concatenate([finished, lane_row(step_last)], axis=1)))
    value_sum = returned[:, :head_count]
    solution = solution + returned[:, head_count, :head_count][:, :, None] * direction
    shared_out = weight_col * value_sum + own_matvec(own_values, solution)
    readout = decay_col * shared_out + write_col * value_now * jnp.sum(
        key_now * solution, axis=2, keepdims=True
    )
    normalized = (
        readout * lax.rsqrt(jnp.mean(readout * readout, axis=2, keepdims=True) + epsilon)
    ).astype(jnp.bfloat16)
    partial_value = jnp.dot(
        normalized.reshape(row_count, head_count * head_size),
        out_weight.reshape(head_count * head_size, model_width),
        preferred_element_type=jnp.float32,
    )
    head_peers = lax.axis_size("head")
    if head_peers == 2:
        me = lax.axis_index("head")
        width = model_width // 2
        mine = lax.dynamic_slice_in_dim(partial_value, me * width, width, axis=1)
        theirs = lax.dynamic_slice_in_dim(partial_value, (1 - me) * width, width, axis=1)
        attended = mine + lax.ppermute(theirs, "head", [(0, 1), (1, 0)])
    else:
        attended = lax.psum_scatter(
            partial_value.astype(jnp.bfloat16), "head", scatter_dimension=1, tiled=True
        ).astype(jnp.float32)
    widened_own = hidden.astype(jnp.float32)
    combined = jnp.where(mask_of_live[:, None], widened_own + attended, widened_own)
    return combined.astype(jnp.bfloat16)


def solution(mesh):
    in_specs = (
        P("req", "head"),
        P(),
        P(None, "head", None, None),
        P(None, "head", None, None),
        P("req", None, "head", None, None),
        P(None, None, "head"),
        P("req", "head"),
        P("head"),
        P("req", "head", None, None),
        P("req", "head", None, None),
        P("req", "head", None, None),
        P("req", "head", None, None),
        P("req"),
        P("req"),
        P("head", None, None),
    )
    out_specs = P("req", "head")
    return jax.shard_map(
        on_device, mesh=mesh, in_specs=in_specs, out_specs=out_specs, check_vma=False
    )
```

```python
import jax
import jax.numpy as jnp
from jax import lax
from jax.sharding import PartitionSpec as P

KW = 4
ITERS = 8
CAP = 6


epsilon = 1e-06
highest = lax.Precision.HIGHEST


def own_matvec(matrices, vectors):
    return jnp.sum(matrices * vectors[:, :, None, :], axis=3)


def on_device(
    hidden,
    norm_gain,
    qkv_weight,
    conv_weight,
    conv_state,
    gate_weight,
    prompt_weight,
    ridge_term,
    own_keys,
    own_values,
    prompt_keys,
    prompt_values,
    group_ids,
    lengths,
    out_weight,
):
    gathered = lax.all_gather(hidden, "head", axis=1, tiled=True)
    widened = gathered.astype(jnp.float32)
    scaled = (
        widened
        * lax.rsqrt(jnp.mean(widened * widened, axis=1, keepdims=True) + epsilon)
        * norm_gain
    )
    normed = scaled.astype(jnp.bfloat16)
    row_count, model_width = gathered.shape
    head_count = qkv_weight.shape[1]
    head_size = qkv_weight.shape[3]
    projected = jnp.dot(
        normed,
        qkv_weight.reshape(model_width, head_count * 3 * head_size),
        preferred_element_type=jnp.float32,
    ).reshape(row_count, head_count, 3, head_size)
    mixing = conv_weight[0] * projected
    for offset in range(1, KW):
        usable = (lengths >= offset).astype(jnp.float32)[:, None, None, None]
        mixing = (
            mixing + conv_weight[offset] * conv_state[:, offset - 1].astype(jnp.float32) * usable
        )
    active = jax.nn.silu(mixing)
    queries = active[:, :, 0]
    queries = queries * lax.rsqrt(jnp.sum(queries * queries, axis=2, keepdims=True) + epsilon)
    key_now = active[:, :, 1]
    key_now = key_now * lax.rsqrt(jnp.sum(key_now * key_now, axis=2, keepdims=True) + epsilon)
    value_now = active[:, :, 2]
    gate_logit = jnp.dot(
        normed, gate_weight.reshape(model_width, 2 * head_count), preferred_element_type=jnp.float32
    ).reshape(row_count, 2, head_count)
    decay_col = jax.nn.sigmoid(gate_logit[:, 0])[:, :, None]
    write_col = jax.nn.sigmoid(gate_logit[:, 1])[:, :, None]
    weight_col = prompt_weight[:, :, None]
    ridge_col = ridge_term[None, :, None]

    peer_count = lax.axis_size("req")
    group_count = prompt_keys.shape[0]
    capacity = CAP
    run_count = row_count // capacity
    slot_count = peer_count * capacity
    mask_of_live = lengths > 0
    owner_of = group_ids // group_count
    local_group = group_ids % group_count
    run_live = jnp.any(mask_of_live.reshape(run_count, capacity), axis=1)
    run_owner = jnp.max(
        jnp.where(mask_of_live, owner_of, -1).reshape(run_count, capacity), axis=1
    )
    claims = (run_owner[:, None] == jnp.arange(peer_count)[None, :]) & run_live[:, None]
    run_ids = jnp.arange(run_count)
    run_of_peer = jnp.sum(jnp.where(claims, run_ids[:, None], 0), axis=0) + jnp.where(
        jnp.any(claims, axis=0), 0, run_count
    )
    peer_of_run = jnp.where(run_live, run_owner, 0)
    slot_label = jnp.where(mask_of_live, local_group + 1, 0)
    live_col = mask_of_live[:, None, None]

    def pack(vectors):
        runs = vectors.reshape((run_count, capacity) + vectors.shape[1:])
        padded = jnp.concatenate([runs, jnp.zeros((1,) + runs.shape[1:], runs.dtype)], axis=0)
        taken = jnp.take(padded, run_of_peer, axis=0, mode="clip")
        return taken.reshape((slot_count,) + vectors.shape[1:])

    def exchange(slots):
        shaped = slots.reshape((peer_count, capacity) + slots.shape[1:])
        moved = lax.all_to_all(shaped, "req", split_axis=0, concat_axis=0, tiled=True)
        return moved.reshape(slots.shape)

    def unpack(slots):
        shaped = slots.reshape((peer_count, capacity) + slots.shape[1:])
        taken = jnp.take(shaped, peer_of_run, axis=0, mode="clip")
        return jnp.where(live_col, taken.reshape((row_count,) + slots.shape[1:]), 0.0)

    def owner_apply(states, incoming, chosen):
        split = jnp.stack(
            [jnp.where(chosen[group][:, None, None], incoming, 0.0) for group in range(group_count)]
        )
        return jnp.einsum("gshj,ghij->shi", split, states, precision=highest)

    def lane_row(values):
        return jnp.pad(values, ((0, 0), (0, head_size - values.shape[1])))[:, None, :]

    def requester_step(shares, solution, residual, direction, norm_now):
        shared = weight_col * shares + own_matvec(own_keys, direction)
        product = (
            decay_col * shared
            + write_col * key_now * jnp.sum(key_now * direction, axis=2, keepdims=True)
            + ridge_col * direction
        )
        step_size = norm_now / jnp.sum(direction * product, axis=2, keepdims=True)
        solution = solution + step_size * direction
        residual = residual - step_size * product
        norm_next = jnp.sum(residual * residual, axis=2, keepdims=True)
        direction = residual + norm_next / norm_now * direction
        return solution, residual, direction, norm_next, step_size

    label_row = lane_row(pack(slot_label.astype(jnp.float32)[:, None]))
    first = exchange(jnp.concatenate([pack(queries), label_row], axis=1))
    labels_in = first[:, head_count, 0]
    chosen = [labels_in == float(group + 1) for group in range(group_count)]
    slot_used = labels_in > 0.5
    held = first[:, :head_count]
    shares = unpack(exchange(owner_apply(prompt_keys, held, chosen)))
    norm_first = jnp.sum(queries * queries, axis=2, keepdims=True)
    solution, residual, direction, norm_now, step_size = requester_step(
        shares, jnp.zeros_like(queries), queries, queries, norm_first
    )
    kept = jnp.zeros((ITERS - 1,) + held.shape, held.dtype).at[0].set(held)
    steps = jnp.zeros((ITERS - 1,) + step_size.shape[:2], step_size.dtype).at[0].set(
        step_size[:, :, 0]
    )

    def middle_step(index, carry):
        solution, residual, direction, norm_now, kept, steps = carry
        arrived = exchange(pack(direction))
        kept = lax.dynamic_update_index_in_dim(kept, arrived, index, 0)
        shares = unpack(exchange(owner_apply(prompt_keys, arrived, chosen)))
        solution, residual, direction, norm_now, step_size = requester_step(
            shares, solution, residual, direction, norm_now
        )
        steps = lax.dynamic_update_index_in_dim(steps, step_size[:, :, 0], index, 0)
        return solution, residual, direction, norm_now, kept, steps

    solution, residual, direction, norm_now, kept, steps = lax.fori_loop(
        1, ITERS - 1, middle_step, (solution, residual, direction, norm_now, kept, steps)
    )

    local_part = (
        decay_col * own_matvec(own_keys, direction)
        + write_col * key_now * jnp.sum(key_now * direction, axis=2, keepdims=True)
        + ridge_col * direction
    )
    local_curve = jnp.sum(direction * local_part, axis=2)
    scalars = jnp.concatenate(
        [jnp.transpose(steps, (1, 0, 2)).reshape(row_count, -1), norm_now[:, :, 0], local_curve,
         (decay_col * weight_col)[:, :, 0]],
        axis=1,
    )
    arrived = exchange(jnp.concatenate([pack(direction), lane_row(pack(scalars))], axis=1))
    extra = arrived[:, head_count]
    held = arrived[:, :head_count]
    known = (ITERS - 1) * head_count
    steps_in = jnp.transpose(extra[:, :known].reshape(slot_count, ITERS - 1, head_count), (1, 0, 2))
    running = jnp.sum(steps_in[:, :, :, None] * kept, axis=0)
    prompt_part = owner_apply(prompt_keys, held, chosen)
    prompt_curve = jnp.sum(held * prompt_part, axis=2)
    rr_in = extra[:, known : known + head_count]
    curve = extra[:, known + head_count : known + 2 * head_count] + extra[
        :, known + 2 * head_count : known + 3 * head_count
    ] * prompt_curve
    step_last = jnp.where(slot_used[:, None], rr_in / jnp.where(slot_used[:, None], curve, 1.0), 0.0)
    running = running + step_last[:, :, None] * held
    finished = owner_apply(prompt_values, running, chosen)
    returned = unpack(exchange(jnp.concatenate([finished, lane_row(step_last)], axis=1)))
    value_sum = returned[:, :head_count]
    solution = solution + returned[:, head_count, :head_count][:, :, None] * direction
    shared_out = weight_col * value_sum + own_matvec(own_values, solution)
    readout = decay_col * shared_out + write_col * value_now * jnp.sum(
        key_now * solution, axis=2, keepdims=True
    )
    normalized = (
        readout * lax.rsqrt(jnp.mean(readout * readout, axis=2, keepdims=True) + epsilon)
    ).astype(jnp.bfloat16)
    partial_value = jnp.dot(
        normalized.reshape(row_count, head_count * head_size),
        out_weight.reshape(head_count * head_size, model_width),
        preferred_element_type=jnp.float32,
    )
    head_peers = lax.axis_size("head")
    if head_peers == 2:
        me = lax.axis_index("head")
        width = model_width // 2
        mine = lax.dynamic_slice_in_dim(partial_value, me * width, width, axis=1)
        theirs = lax.dynamic_slice_in_dim(partial_value, (1 - me) * width, width, axis=1)
        attended = mine + lax.ppermute(theirs, "head", [(0, 1), (1, 0)])
    else:
        attended = lax.psum_scatter(
            partial_value.astype(jnp.bfloat16), "head", scatter_dimension=1, tiled=True
        ).astype(jnp.float32)
    widened_own = hidden.astype(jnp.float32)
    combined = jnp.where(mask_of_live[:, None], widened_own + attended, widened_own)
    return combined.astype(jnp.bfloat16)


def solution(mesh):
    in_specs = (
        P("req", "head"),
        P(),
        P(None, "head", None, None),
        P(None, "head", None, None),
        P("req", None, "head", None, None),
        P(None, None, "head"),
        P("req", "head"),
        P("head"),
        P("req", "head", None, None),
        P("req", "head", None, None),
        P("req", "head", None, None),
        P("req", "head", None, None),
        P("req"),
        P("req"),
        P("head", None, None),
    )
    out_specs = P("req", "head")
    return jax.shard_map(
        on_device, mesh=mesh, in_specs=in_specs, out_specs=out_specs, check_vma=False
    )
```

```python
import jax
import jax.numpy as jnp
from jax import lax
from jax.sharding import PartitionSpec as P

KW = 4
ITERS = 8
CAP = 6


epsilon = 1e-06
highest = lax.Precision.HIGHEST


def own_matvec(matrices, vectors):
    return jnp.sum(matrices * vectors[:, :, None, :], axis=3)


def on_device(
    hidden,
    norm_gain,
    qkv_weight,
    conv_weight,
    conv_state,
    gate_weight,
    prompt_weight,
    ridge_term,
    own_keys,
    own_values,
    prompt_keys,
    prompt_values,
    group_ids,
    lengths,
    out_weight,
):
    gathered = lax.all_gather(hidden, "head", axis=1, tiled=True)
    widened = gathered.astype(jnp.float32)
    scaled = (
        widened
        * lax.rsqrt(jnp.mean(widened * widened, axis=1, keepdims=True) + epsilon)
        * norm_gain
    )
    normed = scaled.astype(jnp.bfloat16)
    row_count, model_width = gathered.shape
    head_count = qkv_weight.shape[1]
    head_size = qkv_weight.shape[3]
    projected = jnp.dot(
        normed,
        qkv_weight.reshape(model_width, head_count * 3 * head_size),
        preferred_element_type=jnp.float32,
    ).reshape(row_count, head_count, 3, head_size)
    mixing = conv_weight[0] * projected
    for offset in range(1, KW):
        usable = (lengths >= offset).astype(jnp.float32)[:, None, None, None]
        mixing = (
            mixing + conv_weight[offset] * conv_state[:, offset - 1].astype(jnp.float32) * usable
        )
    active = jax.nn.silu(mixing)
    queries = active[:, :, 0]
    queries = queries * lax.rsqrt(jnp.sum(queries * queries, axis=2, keepdims=True) + epsilon)
    key_now = active[:, :, 1]
    key_now = key_now * lax.rsqrt(jnp.sum(key_now * key_now, axis=2, keepdims=True) + epsilon)
    value_now = active[:, :, 2]
    gate_logit = jnp.dot(
        normed, gate_weight.reshape(model_width, 2 * head_count), preferred_element_type=jnp.float32
    ).reshape(row_count, 2, head_count)
    decay_col = jax.nn.sigmoid(gate_logit[:, 0])[:, :, None]
    write_col = jax.nn.sigmoid(gate_logit[:, 1])[:, :, None]
    weight_col = prompt_weight[:, :, None]
    ridge_col = ridge_term[None, :, None]

    peer_count = lax.axis_size("req")
    group_count = prompt_keys.shape[0]
    capacity = CAP
    slot_count = peer_count * capacity
    mask_of_live = lengths > 0
    owner_of = group_ids // group_count
    local_group = group_ids % group_count
    order_ids = jnp.arange(row_count)
    earlier = (
        (order_ids[None, :] < order_ids[:, None])
        & (owner_of[None, :] == owner_of[:, None])
        & mask_of_live[None, :]
    )
    rank_of = jnp.sum(earlier.astype(jnp.int32), axis=1)
    routed = mask_of_live & (rank_of < capacity)
    slot_of = jnp.where(routed, owner_of * capacity + rank_of, 0)
    hits = (slot_of[:, None] == jnp.arange(slot_count)[None, :]) & routed[:, None]
    filled = jnp.any(hits, axis=0)
    source = jnp.sum(jnp.where(hits, order_ids[:, None], 0), axis=0) + jnp.where(
        filled, 0, row_count
    )
    slot_label = jnp.sum(jnp.where(hits, (local_group + 1)[:, None], 0), axis=0)

    def pack(vectors):
        padded = jnp.concatenate(
            [vectors, jnp.zeros((1,) + vectors.shape[1:], vectors.dtype)], axis=0
        )
        return jnp.take(padded, source, axis=0)

    def exchange(slots):
        shaped = slots.reshape((peer_count, capacity) + slots.shape[1:])
        moved = lax.all_to_all(shaped, "req", split_axis=0, concat_axis=0, tiled=True)
        return moved.reshape(slots.shape)

    def unpack(slots):
        taken = jnp.take(slots, slot_of, axis=0)
        return jnp.where(routed[:, None, None], taken, 0.0)

    def owner_apply(states, incoming, chosen):
        split = jnp.stack(
            [jnp.where(chosen[group][:, None, None], incoming, 0.0) for group in range(group_count)]
        )
        return jnp.einsum("gshj,ghij->shi", split, states, precision=highest)

    def cg_step(arrived, carry):
        solution, residual, direction, norm_now = carry
        shares = unpack(exchange(owner_apply(prompt_keys, arrived, chosen)))
        shared = weight_col * shares + own_matvec(own_keys, direction)
        product = (
            decay_col * shared
            + write_col * key_now * jnp.sum(key_now * direction, axis=2, keepdims=True)
            + ridge_col * direction
        )
        step_size = norm_now / jnp.sum(direction * product, axis=2, keepdims=True)
        solution = solution + step_size * direction
        residual = residual - step_size * product
        norm_next = jnp.sum(residual * residual, axis=2, keepdims=True)
        direction = residual + norm_next / norm_now * direction
        return solution, residual, direction, norm_next

    label_row = jnp.broadcast_to(
        slot_label.astype(jnp.float32)[:, None, None], (slot_count, 1, head_size)
    )
    first = exchange(jnp.concatenate([pack(queries), label_row], axis=1))
    labels_in = first[:, head_count, 0]
    chosen = [labels_in == float(group + 1) for group in range(group_count)]
    carry = (
        jnp.zeros_like(queries),
        queries,
        queries,
        jnp.sum(queries * queries, axis=2, keepdims=True),
    )
    carry = cg_step(first[:, :head_count], carry)
    carry = lax.fori_loop(
        1, ITERS - 1, lambda _, state: cg_step(exchange(pack(state[2])), state), carry
    )
    solution, residual, direction, norm_now = carry

    local_part = (
        decay_col * own_matvec(own_keys, direction)
        + write_col * key_now * jnp.sum(key_now * direction, axis=2, keepdims=True)
        + ridge_col * direction
    )
    scalars = jnp.concatenate(
        [norm_now[:, :, 0], jnp.sum(direction * local_part, axis=2), (decay_col * weight_col)[:, :, 0]],
        axis=1,
    )
    scalar_row = jnp.pad(scalars, ((0, 0), (0, head_size - scalars.shape[1])))[:, None, :]
    arrived = exchange(jnp.concatenate([pack(direction), pack(solution), pack(scalar_row)], axis=1))
    held = arrived[:, :head_count]
    partial = arrived[:, head_count : 2 * head_count]
    extra = arrived[:, 2 * head_count]
    prompt_curve = jnp.sum(held * owner_apply(prompt_keys, held, chosen), axis=2)
    curve = extra[:, head_count : 2 * head_count] + extra[:, 2 * head_count : 3 * head_count] * prompt_curve
    slot_used = labels_in > 0.5
    step_last = jnp.where(
        slot_used[:, None], extra[:, :head_count] / jnp.where(slot_used[:, None], curve, 1.0), 0.0
    )
    finished = owner_apply(prompt_values, partial + step_last[:, :, None] * held, chosen)
    step_row = jnp.pad(step_last, ((0, 0), (0, head_size - head_count)))[:, None, :]
    returned = unpack(exchange(jnp.concatenate([finished, step_row], axis=1)))
    value_sum = returned[:, :head_count]
    solution = solution + returned[:, head_count, :head_count][:, :, None] * direction
    shared_out = weight_col * value_sum + own_matvec(own_values, solution)
    readout = decay_col * shared_out + write_col * value_now * jnp.sum(
        key_now * solution, axis=2, keepdims=True
    )
    normalized = (
        readout * lax.rsqrt(jnp.mean(readout * readout, axis=2, keepdims=True) + epsilon)
    ).astype(jnp.bfloat16)
    partial_value = jnp.dot(
        normalized.reshape(row_count, head_count * head_size),
        out_weight.reshape(head_count * head_size, model_width),
        preferred_element_type=jnp.float32,
    )
    head_peers = lax.axis_size("head")
    if head_peers == 2:
        me = lax.axis_index("head")
        width = model_width // 2
        mine = lax.dynamic_slice_in_dim(partial_value, me * width, width, axis=1)
        theirs = lax.dynamic_slice_in_dim(partial_value, (1 - me) * width, width, axis=1)
        attended = mine + lax.ppermute(theirs, "head", [(0, 1), (1, 0)])
    else:
        attended = lax.psum_scatter(
            partial_value.astype(jnp.bfloat16), "head", scatter_dimension=1, tiled=True
        ).astype(jnp.float32)
    widened_own = hidden.astype(jnp.float32)
    combined = jnp.where(mask_of_live[:, None], widened_own + attended, widened_own)
    return combined.astype(jnp.bfloat16)


def solution(mesh):
    in_specs = (
        P("req", "head"),
        P(),
        P(None, "head", None, None),
        P(None, "head", None, None),
        P("req", None, "head", None, None),
        P(None, None, "head"),
        P("req", "head"),
        P("head"),
        P("req", "head", None, None),
        P("req", "head", None, None),
        P("req", "head", None, None),
        P("req", "head", None, None),
        P("req"),
        P("req"),
        P("head", None, None),
    )
    out_specs = P("req", "head")
    return jax.shard_map(
        on_device, mesh=mesh, in_specs=in_specs, out_specs=out_specs, check_vma=False
    )
```

```python
import jax
import jax.numpy as jnp
from jax import lax
from jax.sharding import PartitionSpec as P

KW = 4
ITERS = 8
CAP = 6


epsilon = 1e-06
highest = lax.Precision.HIGHEST


def own_matvec(matrices, vectors):
    return jnp.sum(matrices * vectors[:, :, None, :], axis=3)


def on_device(
    hidden,
    norm_gain,
    qkv_weight,
    conv_weight,
    conv_state,
    gate_weight,
    prompt_weight,
    ridge_term,
    own_keys,
    own_values,
    prompt_keys,
    prompt_values,
    group_ids,
    lengths,
    out_weight,
):
    gathered = lax.all_gather(hidden, "head", axis=1, tiled=True)
    widened = gathered.astype(jnp.float32)
    scaled = (
        widened
        * lax.rsqrt(jnp.mean(widened * widened, axis=1, keepdims=True) + epsilon)
        * norm_gain
    )
    normed = scaled.astype(jnp.bfloat16)
    row_count, model_width = gathered.shape
    head_count = qkv_weight.shape[1]
    head_size = qkv_weight.shape[3]
    live_rows = [(lengths >= offset).astype(jnp.float32)[:, None, None] for offset in range(KW)]

    def project(part):
        weights = qkv_weight[:, :, part, :].reshape(model_width, head_count * head_size)
        mixing = conv_weight[0, :, part] * jnp.dot(
            normed, weights, preferred_element_type=jnp.float32
        ).reshape(row_count, head_count, head_size)
        for offset in range(1, KW):
            mixing = mixing + conv_weight[offset, :, part] * conv_state[
                :, offset - 1, :, part
            ].astype(jnp.float32) * live_rows[offset]
        return jax.nn.silu(mixing)

    queries = project(0)
    queries = queries * lax.rsqrt(jnp.sum(queries * queries, axis=2, keepdims=True) + epsilon)
    key_now = project(1)
    key_now = key_now * lax.rsqrt(jnp.sum(key_now * key_now, axis=2, keepdims=True) + epsilon)
    value_now = project(2)
    gate_logit = jnp.dot(
        normed, gate_weight.reshape(model_width, 2 * head_count), preferred_element_type=jnp.float32
    ).reshape(row_count, 2, head_count)
    decay_col = jax.nn.sigmoid(gate_logit[:, 0])[:, :, None]
    write_col = jax.nn.sigmoid(gate_logit[:, 1])[:, :, None]
    weight_col = prompt_weight[:, :, None]
    ridge_col = ridge_term[None, :, None]

    peer_count = lax.axis_size("req")
    group_count = prompt_keys.shape[0]
    capacity = CAP
    slot_count = peer_count * capacity
    mask_of_live = lengths > 0
    owner_of = group_ids // group_count
    local_group = group_ids % group_count
    order_ids = jnp.arange(row_count)
    earlier = (
        (order_ids[None, :] < order_ids[:, None])
        & (owner_of[None, :] == owner_of[:, None])
        & mask_of_live[None, :]
    )
    rank_of = jnp.sum(earlier.astype(jnp.int32), axis=1)
    routed = mask_of_live & (rank_of < capacity)
    slot_of = jnp.where(routed, owner_of * capacity + rank_of, 0)
    hits = (slot_of[:, None] == jnp.arange(slot_count)[None, :]) & routed[:, None]
    filled = jnp.any(hits, axis=0)
    source = jnp.sum(jnp.where(hits, order_ids[:, None], 0), axis=0) + jnp.where(
        filled, 0, row_count
    )
    slot_label = jnp.sum(jnp.where(hits, (local_group + 1)[:, None], 0), axis=0)

    def pack(vectors):
        padded = jnp.concatenate(
            [vectors, jnp.zeros((1,) + vectors.shape[1:], vectors.dtype)], axis=0
        )
        return jnp.take(padded, source, axis=0)

    def exchange(slots):
        shaped = slots.reshape((peer_count, capacity) + slots.shape[1:])
        moved = lax.all_to_all(shaped, "req", split_axis=0, concat_axis=0, tiled=True)
        return moved.reshape(slots.shape)

    def unpack(slots):
        taken = jnp.take(slots, slot_of, axis=0)
        return jnp.where(routed[:, None, None], taken, 0.0)

    def owner_apply(states, incoming, chosen):
        split = jnp.stack(
            [jnp.where(chosen[group][:, None, None], incoming, 0.0) for group in range(group_count)]
        )
        return jnp.einsum("gshj,ghij->shi", split, states, precision=highest)

    def cg_step(arrived, carry):
        solution, residual, direction, norm_now = carry
        shares = unpack(exchange(owner_apply(prompt_keys, arrived, chosen)))
        shared = weight_col * shares + own_matvec(own_keys, direction)
        product = (
            decay_col * shared
            + write_col * key_now * jnp.sum(key_now * direction, axis=2, keepdims=True)
            + ridge_col * direction
        )
        step_size = norm_now / jnp.sum(direction * product, axis=2, keepdims=True)
        solution = solution + step_size * direction
        residual = residual - step_size * product
        norm_next = jnp.sum(residual * residual, axis=2, keepdims=True)
        direction = residual + norm_next / norm_now * direction
        return solution, residual, direction, norm_next

    label_row = jnp.broadcast_to(
        slot_label.astype(jnp.float32)[:, None, None], (slot_count, 1, head_size)
    )
    first = exchange(jnp.concatenate([pack(queries), label_row], axis=1))
    labels_in = first[:, head_count, 0]
    chosen = [labels_in == float(group + 1) for group in range(group_count)]
    carry = (
        jnp.zeros_like(queries),
        queries,
        queries,
        jnp.sum(queries * queries, axis=2, keepdims=True),
    )
    carry = cg_step(first[:, :head_count], carry)
    carry = lax.fori_loop(
        1, ITERS - 1, lambda _, state: cg_step(exchange(pack(state[2])), state), carry
    )
    solution, residual, direction, norm_now = carry

    local_part = (
        decay_col * own_matvec(own_keys, direction)
        + write_col * key_now * jnp.sum(key_now * direction, axis=2, keepdims=True)
        + ridge_col * direction
    )
    scalars = jnp.concatenate(
        [norm_now[:, :, 0], jnp.sum(direction * local_part, axis=2), (decay_col * weight_col)[:, :, 0]],
        axis=1,
    )
    scalar_row = jnp.pad(scalars, ((0, 0), (0, head_size - scalars.shape[1])))[:, None, :]
    arrived = exchange(jnp.concatenate([pack(direction), pack(solution), pack(scalar_row)], axis=1))
    held = arrived[:, :head_count]
    partial = arrived[:, head_count : 2 * head_count]
    extra = arrived[:, 2 * head_count]
    prompt_curve = jnp.sum(held * owner_apply(prompt_keys, held, chosen), axis=2)
    curve = extra[:, head_count : 2 * head_count] + extra[:, 2 * head_count : 3 * head_count] * prompt_curve
    slot_used = labels_in > 0.5
    step_last = jnp.where(
        slot_used[:, None], extra[:, :head_count] / jnp.where(slot_used[:, None], curve, 1.0), 0.0
    )
    finished = owner_apply(prompt_values, partial + step_last[:, :, None] * held, chosen)
    step_row = jnp.pad(step_last, ((0, 0), (0, head_size - head_count)))[:, None, :]
    returned = unpack(exchange(jnp.concatenate([finished, step_row], axis=1)))
    value_sum = returned[:, :head_count]
    solution = solution + returned[:, head_count, :head_count][:, :, None] * direction
    shared_out = weight_col * value_sum + own_matvec(own_values, solution)
    readout = decay_col * shared_out + write_col * value_now * jnp.sum(
        key_now * solution, axis=2, keepdims=True
    )
    normalized = (
        readout * lax.rsqrt(jnp.mean(readout * readout, axis=2, keepdims=True) + epsilon)
    ).astype(jnp.bfloat16)
    partial_value = jnp.dot(
        normalized.reshape(row_count, head_count * head_size),
        out_weight.reshape(head_count * head_size, model_width),
        preferred_element_type=jnp.float32,
    )
    head_peers = lax.axis_size("head")
    if head_peers == 2:
        me = lax.axis_index("head")
        width = model_width // 2
        mine = lax.dynamic_slice_in_dim(partial_value, me * width, width, axis=1)
        theirs = lax.dynamic_slice_in_dim(partial_value, (1 - me) * width, width, axis=1)
        attended = mine + lax.ppermute(theirs, "head", [(0, 1), (1, 0)])
    else:
        attended = lax.psum_scatter(
            partial_value.astype(jnp.bfloat16), "head", scatter_dimension=1, tiled=True
        ).astype(jnp.float32)
    widened_own = hidden.astype(jnp.float32)
    combined = jnp.where(mask_of_live[:, None], widened_own + attended, widened_own)
    return combined.astype(jnp.bfloat16)


def solution(mesh):
    in_specs = (
        P("req", "head"),
        P(),
        P(None, "head", None, None),
        P(None, "head", None, None),
        P("req", None, "head", None, None),
        P(None, None, "head"),
        P("req", "head"),
        P("head"),
        P("req", "head", None, None),
        P("req", "head", None, None),
        P("req", "head", None, None),
        P("req", "head", None, None),
        P("req"),
        P("req"),
        P("head", None, None),
    )
    out_specs = P("req", "head")
    return jax.shard_map(
        on_device, mesh=mesh, in_specs=in_specs, out_specs=out_specs, check_vma=False
    )
```

```python
import jax
import jax.numpy as jnp
from jax import lax
from jax.sharding import PartitionSpec as P

KW = 4
ITERS = 8
CAP = 6


epsilon = 1e-06
highest = lax.Precision.HIGHEST


def own_matvec(matrices, vectors):
    return jnp.sum(matrices * vectors[:, :, None, :], axis=3)


def on_device(
    hidden,
    norm_gain,
    qkv_weight,
    conv_weight,
    conv_state,
    gate_weight,
    prompt_weight,
    ridge_term,
    own_keys,
    own_values,
    prompt_keys,
    prompt_values,
    group_ids,
    lengths,
    out_weight,
):
    gathered = lax.all_gather(hidden, "head", axis=1, tiled=True)
    widened = gathered.astype(jnp.float32)
    scaled = (
        widened
        * lax.rsqrt(jnp.mean(widened * widened, axis=1, keepdims=True) + epsilon)
        * norm_gain
    )
    normed = scaled.astype(jnp.bfloat16)
    row_count, model_width = gathered.shape
    head_count = qkv_weight.shape[1]
    head_size = qkv_weight.shape[3]
    projected = jnp.dot(
        normed,
        qkv_weight.reshape(model_width, head_count * 3 * head_size),
        preferred_element_type=jnp.float32,
    ).reshape(row_count, head_count, 3, head_size)
    mixing = conv_weight[0] * projected
    for offset in range(1, KW):
        usable = (lengths >= offset).astype(jnp.float32)[:, None, None, None]
        mixing = (
            mixing + conv_weight[offset] * conv_state[:, offset - 1].astype(jnp.float32) * usable
        )
    active = jax.nn.silu(mixing)
    queries = active[:, :, 0]
    queries = queries * lax.rsqrt(jnp.sum(queries * queries, axis=2, keepdims=True) + epsilon)
    key_now = active[:, :, 1]
    key_now = key_now * lax.rsqrt(jnp.sum(key_now * key_now, axis=2, keepdims=True) + epsilon)
    value_now = active[:, :, 2]
    gate_logit = jnp.dot(
        normed, gate_weight.reshape(model_width, 2 * head_count), preferred_element_type=jnp.float32
    ).reshape(row_count, 2, head_count)
    decay_col = jax.nn.sigmoid(gate_logit[:, 0])[:, :, None]
    write_col = jax.nn.sigmoid(gate_logit[:, 1])[:, :, None]
    weight_col = prompt_weight[:, :, None]
    ridge_col = ridge_term[None, :, None]

    peer_count = lax.axis_size("req")
    group_count = prompt_keys.shape[0]
    capacity = CAP
    slot_count = peer_count * capacity
    mask_of_live = lengths > 0
    owner_of = group_ids // group_count
    local_group = group_ids % group_count
    order_ids = jnp.arange(row_count)
    earlier = (
        (order_ids[None, :] < order_ids[:, None])
        & (owner_of[None, :] == owner_of[:, None])
        & mask_of_live[None, :]
    )
    rank_of = jnp.sum(earlier.astype(jnp.int32), axis=1)
    routed = mask_of_live & (rank_of < capacity)
    slot_of = jnp.where(routed, owner_of * capacity + rank_of, 0)
    hits = (slot_of[:, None] == jnp.arange(slot_count)[None, :]) & routed[:, None]
    filled = jnp.any(hits, axis=0)
    source = jnp.sum(jnp.where(hits, order_ids[:, None], 0), axis=0) + jnp.where(
        filled, 0, row_count
    )
    slot_label = jnp.sum(jnp.where(hits, (local_group + 1)[:, None], 0), axis=0)

    def pack(vectors):
        padded = jnp.concatenate(
            [vectors, jnp.zeros((1,) + vectors.shape[1:], vectors.dtype)], axis=0
        )
        return jnp.take(padded, source, axis=0)

    def exchange(slots):
        shaped = slots.reshape((peer_count, capacity) + slots.shape[1:])
        moved = lax.all_to_all(shaped, "req", split_axis=0, concat_axis=0, tiled=True)
        return moved.reshape(slots.shape)

    def unpack(slots):
        taken = jnp.take(slots, slot_of, axis=0)
        return jnp.where(routed[:, None, None], taken, 0.0)

    def owner_apply(states, incoming, chosen):
        products = jnp.einsum("shj,ghij->gshi", incoming, states, precision=highest)
        total = jnp.where(chosen[0][:, None, None], products[0], 0.0)
        for group in range(1, group_count):
            total = total + jnp.where(chosen[group][:, None, None], products[group], 0.0)
        return total

    def cg_step(arrived, carry):
        solution, residual, direction, norm_now = carry
        shares = unpack(exchange(owner_apply(prompt_keys, arrived, chosen)))
        shared = weight_col * shares + own_matvec(own_keys, direction)
        product = (
            decay_col * shared
            + write_col * key_now * jnp.sum(key_now * direction, axis=2, keepdims=True)
            + ridge_col * direction
        )
        step_size = norm_now / jnp.sum(direction * product, axis=2, keepdims=True)
        solution = solution + step_size * direction
        residual = residual - step_size * product
        norm_next = jnp.sum(residual * residual, axis=2, keepdims=True)
        direction = residual + norm_next / norm_now * direction
        return solution, residual, direction, norm_next

    label_row = jnp.broadcast_to(
        slot_label.astype(jnp.float32)[:, None, None], (slot_count, 1, head_size)
    )
    first = exchange(jnp.concatenate([pack(queries), label_row], axis=1))
    labels_in = first[:, head_count, 0]
    chosen = [labels_in == float(group + 1) for group in range(group_count)]
    carry = (
        jnp.zeros_like(queries),
        queries,
        queries,
        jnp.sum(queries * queries, axis=2, keepdims=True),
    )
    carry = cg_step(first[:, :head_count], carry)
    carry = lax.fori_loop(
        1, ITERS - 1, lambda _, state: cg_step(exchange(pack(state[2])), state), carry
    )
    solution, residual, direction, norm_now = carry

    both = exchange(jnp.concatenate([pack(direction), pack(solution)], axis=1))
    held = both[:, :head_count]
    owner_out = jnp.concatenate(
        [
            owner_apply(prompt_keys, held, chosen),
            owner_apply(prompt_values, both[:, head_count:], chosen),
            owner_apply(prompt_values, held, chosen),
        ],
        axis=1,
    )
    returned = unpack(exchange(owner_out))
    own_out_partial = own_matvec(own_values, solution)
    own_out_direction = own_matvec(own_values, direction)
    partial = solution
    shares = returned[:, :head_count]
    shared = weight_col * shares + own_matvec(own_keys, direction)
    product = (
        decay_col * shared
        + write_col * key_now * jnp.sum(key_now * direction, axis=2, keepdims=True)
        + ridge_col * direction
    )
    step_last = norm_now / jnp.sum(direction * product, axis=2, keepdims=True)
    solution = partial + step_last * direction
    value_sum = returned[:, head_count : 2 * head_count] + step_last * returned[:, 2 * head_count :]
    own_out = own_out_partial + step_last * own_out_direction
    shared_out = weight_col * value_sum + own_out
    readout = decay_col * shared_out + write_col * value_now * jnp.sum(
        key_now * solution, axis=2, keepdims=True
    )
    normalized = (
        readout * lax.rsqrt(jnp.mean(readout * readout, axis=2, keepdims=True) + epsilon)
    ).astype(jnp.bfloat16)
    partial_value = jnp.dot(
        normalized.reshape(row_count, head_count * head_size),
        out_weight.reshape(head_count * head_size, model_width),
        preferred_element_type=jnp.float32,
    )
    head_peers = lax.axis_size("head")
    if head_peers == 2:
        me = lax.axis_index("head")
        width = model_width // 2
        mine = lax.dynamic_slice_in_dim(partial_value, me * width, width, axis=1)
        theirs = lax.dynamic_slice_in_dim(partial_value, (1 - me) * width, width, axis=1)
        attended = mine + lax.ppermute(theirs, "head", [(0, 1), (1, 0)])
    else:
        attended = lax.psum_scatter(
            partial_value.astype(jnp.bfloat16), "head", scatter_dimension=1, tiled=True
        ).astype(jnp.float32)
    widened_own = hidden.astype(jnp.float32)
    combined = jnp.where(mask_of_live[:, None], widened_own + attended, widened_own)
    return combined.astype(jnp.bfloat16)


def solution(mesh):
    in_specs = (
        P("req", "head"),
        P(),
        P(None, "head", None, None),
        P(None, "head", None, None),
        P("req", None, "head", None, None),
        P(None, None, "head"),
        P("req", "head"),
        P("head"),
        P("req", "head", None, None),
        P("req", "head", None, None),
        P("req", "head", None, None),
        P("req", "head", None, None),
        P("req"),
        P("req"),
        P("head", None, None),
    )
    out_specs = P("req", "head")
    return jax.shard_map(
        on_device, mesh=mesh, in_specs=in_specs, out_specs=out_specs, check_vma=False
    )
```

```python
import jax
import jax.numpy as jnp
from jax import lax
from jax.sharding import PartitionSpec as P

KW = 4
ITERS = 8
CAP = 6


epsilon = 1e-06
highest = lax.Precision.HIGHEST


def own_matvec(matrices, vectors):
    return jnp.sum(matrices * vectors[:, :, None, :], axis=3)


def on_device(
    hidden,
    norm_gain,
    qkv_weight,
    conv_weight,
    conv_state,
    gate_weight,
    prompt_weight,
    ridge_term,
    own_keys,
    own_values,
    prompt_keys,
    prompt_values,
    group_ids,
    lengths,
    out_weight,
):
    gathered = lax.all_gather(hidden, "head", axis=1, tiled=True)
    widened = gathered.astype(jnp.float32)
    scaled = (
        widened
        * lax.rsqrt(jnp.mean(widened * widened, axis=1, keepdims=True) + epsilon)
        * norm_gain
    )
    normed = scaled.astype(jnp.bfloat16)
    row_count, model_width = gathered.shape
    head_count = qkv_weight.shape[1]
    head_size = qkv_weight.shape[3]
    projected = jnp.dot(
        normed,
        qkv_weight.reshape(model_width, head_count * 3 * head_size),
        preferred_element_type=jnp.float32,
    ).reshape(row_count, head_count, 3, head_size)
    mixing = conv_weight[0] * projected
    for offset in range(1, KW):
        usable = (lengths >= offset).astype(jnp.float32)[:, None, None, None]
        mixing = (
            mixing + conv_weight[offset] * conv_state[:, offset - 1].astype(jnp.float32) * usable
        )
    active = jax.nn.silu(mixing)
    queries = active[:, :, 0]
    queries = queries * lax.rsqrt(jnp.sum(queries * queries, axis=2, keepdims=True) + epsilon)
    key_now = active[:, :, 1]
    key_now = key_now * lax.rsqrt(jnp.sum(key_now * key_now, axis=2, keepdims=True) + epsilon)
    value_now = active[:, :, 2]
    gate_logit = jnp.dot(
        normed, gate_weight.reshape(model_width, 2 * head_count), preferred_element_type=jnp.float32
    ).reshape(row_count, 2, head_count)
    decay_col = jax.nn.sigmoid(gate_logit[:, 0])[:, :, None]
    write_col = jax.nn.sigmoid(gate_logit[:, 1])[:, :, None]
    weight_col = prompt_weight[:, :, None]
    ridge_col = ridge_term[None, :, None]

    peer_count = lax.axis_size("req")
    group_count = prompt_keys.shape[0]
    capacity = CAP
    slot_count = peer_count * capacity
    mask_of_live = lengths > 0
    owner_of = group_ids // group_count
    local_group = group_ids % group_count
    order_ids = jnp.arange(row_count)
    earlier = (
        (order_ids[None, :] < order_ids[:, None])
        & (owner_of[None, :] == owner_of[:, None])
        & mask_of_live[None, :]
    )
    rank_of = jnp.sum(earlier.astype(jnp.int32), axis=1)
    routed = mask_of_live & (rank_of < capacity)
    slot_of = jnp.where(routed, owner_of * capacity + rank_of, 0)
    hits = (slot_of[:, None] == jnp.arange(slot_count)[None, :]) & routed[:, None]
    filled = jnp.any(hits, axis=0)
    source = jnp.sum(jnp.where(hits, order_ids[:, None], 0), axis=0) + jnp.where(
        filled, 0, row_count
    )
    slot_label = jnp.sum(jnp.where(hits, (local_group + 1)[:, None], 0), axis=0)

    def pack(vectors):
        padded = jnp.concatenate(
            [vectors, jnp.zeros((1,) + vectors.shape[1:], vectors.dtype)], axis=0
        )
        return jnp.take(padded, source, axis=0, mode="clip")

    def exchange(slots):
        shaped = slots.reshape((peer_count, capacity) + slots.shape[1:])
        moved = lax.all_to_all(shaped, "req", split_axis=0, concat_axis=0, tiled=True)
        return moved.reshape(slots.shape)

    def unpack(slots):
        taken = jnp.take(slots, slot_of, axis=0, mode="clip")
        return jnp.where(routed[:, None, None], taken, 0.0)

    def owner_apply(states, incoming, chosen):
        products = jnp.einsum("shj,ghij->gshi", incoming, states, precision=highest)
        total = jnp.where(chosen[0][:, None, None], products[0], 0.0)
        for group in range(1, group_count):
            total = total + jnp.where(chosen[group][:, None, None], products[group], 0.0)
        return total

    def cg_step(arrived, carry):
        solution, residual, direction, norm_now = carry
        shares = unpack(exchange(owner_apply(prompt_keys, arrived, chosen)))
        shared = weight_col * shares + own_matvec(own_keys, direction)
        product = (
            decay_col * shared
            + write_col * key_now * jnp.sum(key_now * direction, axis=2, keepdims=True)
            + ridge_col * direction
        )
        step_size = norm_now / jnp.sum(direction * product, axis=2, keepdims=True)
        solution = solution + step_size * direction
        residual = residual - step_size * product
        norm_next = jnp.sum(residual * residual, axis=2, keepdims=True)
        direction = residual + norm_next / norm_now * direction
        return solution, residual, direction, norm_next

    label_row = jnp.broadcast_to(
        slot_label.astype(jnp.float32)[:, None, None], (slot_count, 1, head_size)
    )
    first = exchange(jnp.concatenate([pack(queries), label_row], axis=1))
    labels_in = first[:, head_count, 0]
    chosen = [labels_in == float(group + 1) for group in range(group_count)]
    carry = (
        jnp.zeros_like(queries),
        queries,
        queries,
        jnp.sum(queries * queries, axis=2, keepdims=True),
    )
    carry = cg_step(first[:, :head_count], carry)
    carry = lax.fori_loop(
        1, ITERS - 1, lambda _, state: cg_step(exchange(pack(state[2])), state), carry
    )
    solution, residual, direction, norm_now = carry

    both = exchange(jnp.concatenate([pack(direction), pack(solution)], axis=1))
    held = both[:, :head_count]
    owner_out = jnp.concatenate(
        [
            owner_apply(prompt_keys, held, chosen),
            owner_apply(prompt_values, both[:, head_count:], chosen),
            owner_apply(prompt_values, held, chosen),
        ],
        axis=1,
    )
    returned = unpack(exchange(owner_out))
    own_out_partial = own_matvec(own_values, solution)
    own_out_direction = own_matvec(own_values, direction)
    partial = solution
    shares = returned[:, :head_count]
    shared = weight_col * shares + own_matvec(own_keys, direction)
    product = (
        decay_col * shared
        + write_col * key_now * jnp.sum(key_now * direction, axis=2, keepdims=True)
        + ridge_col * direction
    )
    step_last = norm_now / jnp.sum(direction * product, axis=2, keepdims=True)
    solution = partial + step_last * direction
    value_sum = returned[:, head_count : 2 * head_count] + step_last * returned[:, 2 * head_count :]
    own_out = own_out_partial + step_last * own_out_direction
    shared_out = weight_col * value_sum + own_out
    readout = decay_col * shared_out + write_col * value_now * jnp.sum(
        key_now * solution, axis=2, keepdims=True
    )
    normalized = (
        readout * lax.rsqrt(jnp.mean(readout * readout, axis=2, keepdims=True) + epsilon)
    ).astype(jnp.bfloat16)
    partial_value = jnp.dot(
        normalized.reshape(row_count, head_count * head_size),
        out_weight.reshape(head_count * head_size, model_width),
        preferred_element_type=jnp.float32,
    )
    head_peers = lax.axis_size("head")
    if head_peers == 2:
        me = lax.axis_index("head")
        width = model_width // 2
        mine = lax.dynamic_slice_in_dim(partial_value, me * width, width, axis=1)
        theirs = lax.dynamic_slice_in_dim(partial_value, (1 - me) * width, width, axis=1)
        attended = mine + lax.ppermute(theirs, "head", [(0, 1), (1, 0)])
    else:
        attended = lax.psum_scatter(
            partial_value.astype(jnp.bfloat16), "head", scatter_dimension=1, tiled=True
        ).astype(jnp.float32)
    widened_own = hidden.astype(jnp.float32)
    combined = jnp.where(mask_of_live[:, None], widened_own + attended, widened_own)
    return combined.astype(jnp.bfloat16)


def solution(mesh):
    in_specs = (
        P("req", "head"),
        P(),
        P(None, "head", None, None),
        P(None, "head", None, None),
        P("req", None, "head", None, None),
        P(None, None, "head"),
        P("req", "head"),
        P("head"),
        P("req", "head", None, None),
        P("req", "head", None, None),
        P("req", "head", None, None),
        P("req", "head", None, None),
        P("req"),
        P("req"),
        P("head", None, None),
    )
    out_specs = P("req", "head")
    return jax.shard_map(
        on_device, mesh=mesh, in_specs=in_specs, out_specs=out_specs, check_vma=False
    )
```

```python
import jax
import jax.numpy as jnp
from jax import lax
from jax.sharding import PartitionSpec as P

KW = 4
ITERS = 8
CAP = 6


epsilon = 1e-06
highest = lax.Precision.HIGHEST


def own_matvec(matrices, vectors):
    return jnp.sum(matrices * vectors[:, :, None, :], axis=3)


def on_device(
    hidden,
    norm_gain,
    qkv_weight,
    conv_weight,
    conv_state,
    gate_weight,
    prompt_weight,
    ridge_term,
    own_keys,
    own_values,
    prompt_keys,
    prompt_values,
    group_ids,
    lengths,
    out_weight,
):
    gathered = lax.all_gather(hidden, "head", axis=1, tiled=True)
    widened = gathered.astype(jnp.float32)
    scaled = (
        widened
        * lax.rsqrt(jnp.mean(widened * widened, axis=1, keepdims=True) + epsilon)
        * norm_gain
    )
    normed = scaled.astype(jnp.bfloat16)
    row_count, model_width = gathered.shape
    head_count = qkv_weight.shape[1]
    head_size = qkv_weight.shape[3]
    projected = jnp.dot(
        normed,
        qkv_weight.reshape(model_width, head_count * 3 * head_size),
        preferred_element_type=jnp.float32,
    ).reshape(row_count, head_count, 3, head_size)
    mixing = conv_weight[0] * projected
    for offset in range(1, KW):
        usable = (lengths >= offset).astype(jnp.float32)[:, None, None, None]
        mixing = (
            mixing + conv_weight[offset] * conv_state[:, offset - 1].astype(jnp.float32) * usable
        )
    active = jax.nn.silu(mixing)
    queries = active[:, :, 0]
    queries = queries * lax.rsqrt(jnp.sum(queries * queries, axis=2, keepdims=True) + epsilon)
    key_now = active[:, :, 1]
    key_now = key_now * lax.rsqrt(jnp.sum(key_now * key_now, axis=2, keepdims=True) + epsilon)
    value_now = active[:, :, 2]
    gate_logit = jnp.dot(
        normed, gate_weight.reshape(model_width, 2 * head_count), preferred_element_type=jnp.float32
    ).reshape(row_count, 2, head_count)
    decay_col = jax.nn.sigmoid(gate_logit[:, 0])[:, :, None]
    write_col = jax.nn.sigmoid(gate_logit[:, 1])[:, :, None]
    weight_col = prompt_weight[:, :, None]
    ridge_col = ridge_term[None, :, None]

    peer_count = lax.axis_size("req")
    group_count = prompt_keys.shape[0]
    capacity = CAP
    slot_count = peer_count * capacity
    mask_of_live = lengths > 0
    owner_of = group_ids // group_count
    local_group = group_ids % group_count
    order_ids = jnp.arange(row_count)
    earlier = (
        (order_ids[None, :] < order_ids[:, None])
        & (owner_of[None, :] == owner_of[:, None])
        & mask_of_live[None, :]
    )
    rank_of = jnp.sum(earlier.astype(jnp.int32), axis=1)
    routed = mask_of_live & (rank_of < capacity)
    slot_of = jnp.where(routed, owner_of * capacity + rank_of, 0)
    hits = (slot_of[:, None] == jnp.arange(slot_count)[None, :]) & routed[:, None]
    filled = jnp.any(hits, axis=0)
    source = jnp.sum(jnp.where(hits, order_ids[:, None], 0), axis=0) + jnp.where(
        filled, 0, row_count
    )
    slot_label = jnp.sum(jnp.where(hits, (local_group + 1)[:, None], 0), axis=0)

    def pack(vectors):
        padded = jnp.concatenate(
            [vectors, jnp.zeros((1,) + vectors.shape[1:], vectors.dtype)], axis=0
        )
        return jnp.take(padded, source, axis=0, mode="clip")

    def exchange(slots):
        shaped = slots.reshape((peer_count, capacity) + slots.shape[1:])
        moved = lax.all_to_all(shaped, "req", split_axis=0, concat_axis=0, tiled=True)
        return moved.reshape(slots.shape)

    def unpack(slots):
        taken = jnp.take(slots, slot_of, axis=0, mode="clip")
        return jnp.where(routed[:, None, None], taken, 0.0)

    def owner_apply(states, incoming, chosen):
        products = jnp.einsum("shj,ghij->gshi", incoming, states, precision=highest)
        total = jnp.where(chosen[0][:, None, None], products[0], 0.0)
        for group in range(1, group_count):
            total = total + jnp.where(chosen[group][:, None, None], products[group], 0.0)
        return total

    filled_col = filled[:, None, None]
    queries_s = pack(queries)
    key_s = pack(key_now)
    decay_s = pack(decay_col)
    write_s = pack(write_col)
    weight_s = pack(weight_col)

    def own_in_slots(states, vectors):
        return pack(own_matvec(states, jnp.take(vectors, slot_of, axis=0, mode="clip")))

    def requester_step(shares, own, solution, residual, direction, norm_now):
        product = (
            decay_s * (weight_s * shares + own)
            + write_s * key_s * jnp.sum(key_s * direction, axis=2, keepdims=True)
            + ridge_col * direction
        )
        curve = jnp.sum(direction * product, axis=2, keepdims=True)
        step_size = jnp.where(filled_col, norm_now / jnp.where(filled_col, curve, 1.0), 0.0)
        solution = solution + step_size * direction
        residual = residual - step_size * product
        norm_next = jnp.sum(residual * residual, axis=2, keepdims=True)
        ratio = jnp.where(filled_col, norm_next / jnp.where(filled_col, norm_now, 1.0), 0.0)
        direction = residual + ratio * direction
        return solution, residual, direction, norm_next

    label_row = jnp.broadcast_to(
        slot_label.astype(jnp.float32)[:, None, None], (slot_count, 1, head_size)
    )
    first = exchange(jnp.concatenate([queries_s, label_row], axis=1))
    own_first = own_in_slots(own_keys, queries_s)
    labels_in = first[:, head_count, 0]
    chosen = [labels_in == float(group + 1) for group in range(group_count)]
    shares = exchange(owner_apply(prompt_keys, first[:, :head_count], chosen))
    norm_first = jnp.sum(queries_s * queries_s, axis=2, keepdims=True)
    carry = requester_step(
        shares, own_first, jnp.zeros_like(queries_s), queries_s, queries_s, norm_first
    )

    def middle_step(_, carry):
        solution, residual, direction, norm_now = carry
        arrived = exchange(direction)
        own = own_in_slots(own_keys, direction)
        shares = exchange(owner_apply(prompt_keys, arrived, chosen))
        return requester_step(shares, own, solution, residual, direction, norm_now)

    solution, residual, direction, norm_now = lax.fori_loop(1, ITERS - 1, middle_step, carry)

    both = exchange(jnp.concatenate([direction, solution], axis=1))
    own = own_in_slots(own_keys, direction)
    held = both[:, :head_count]
    owner_out = jnp.concatenate(
        [
            owner_apply(prompt_keys, held, chosen),
            owner_apply(prompt_values, both[:, head_count:], chosen),
            owner_apply(prompt_values, held, chosen),
        ],
        axis=1,
    )
    returned = exchange(owner_out)
    own_out_partial = own_matvec(own_values, unpack(solution))
    own_out_direction = own_matvec(own_values, unpack(direction))
    shares = returned[:, :head_count]
    product = (
        decay_s * (weight_s * shares + own)
        + write_s * key_s * jnp.sum(key_s * direction, axis=2, keepdims=True)
        + ridge_col * direction
    )
    curve = jnp.sum(direction * product, axis=2, keepdims=True)
    step_last = jnp.where(filled_col, norm_now / jnp.where(filled_col, curve, 1.0), 0.0)
    solution = unpack(solution + step_last * direction)
    value_sum = unpack(
        returned[:, head_count : 2 * head_count] + step_last * returned[:, 2 * head_count :]
    )
    own_out = own_out_partial + unpack(step_last) * own_out_direction
    shared_out = weight_col * value_sum + own_out
    readout = decay_col * shared_out + write_col * value_now * jnp.sum(
        key_now * solution, axis=2, keepdims=True
    )
    normalized = (
        readout * lax.rsqrt(jnp.mean(readout * readout, axis=2, keepdims=True) + epsilon)
    ).astype(jnp.bfloat16)
    partial_value = jnp.dot(
        normalized.reshape(row_count, head_count * head_size),
        out_weight.reshape(head_count * head_size, model_width),
        preferred_element_type=jnp.float32,
    )
    head_peers = lax.axis_size("head")
    if head_peers == 2:
        me = lax.axis_index("head")
        width = model_width // 2
        mine = lax.dynamic_slice_in_dim(partial_value, me * width, width, axis=1)
        theirs = lax.dynamic_slice_in_dim(partial_value, (1 - me) * width, width, axis=1)
        attended = mine + lax.ppermute(theirs, "head", [(0, 1), (1, 0)])
    else:
        attended = lax.psum_scatter(
            partial_value.astype(jnp.bfloat16), "head", scatter_dimension=1, tiled=True
        ).astype(jnp.float32)
    widened_own = hidden.astype(jnp.float32)
    combined = jnp.where(mask_of_live[:, None], widened_own + attended, widened_own)
    return combined.astype(jnp.bfloat16)


def solution(mesh):
    in_specs = (
        P("req", "head"),
        P(),
        P(None, "head", None, None),
        P(None, "head", None, None),
        P("req", None, "head", None, None),
        P(None, None, "head"),
        P("req", "head"),
        P("head"),
        P("req", "head", None, None),
        P("req", "head", None, None),
        P("req", "head", None, None),
        P("req", "head", None, None),
        P("req"),
        P("req"),
        P("head", None, None),
    )
    out_specs = P("req", "head")
    return jax.shard_map(
        on_device, mesh=mesh, in_specs=in_specs, out_specs=out_specs, check_vma=False
    )
```

```python
import jax
import jax.numpy as jnp
from jax import lax
from jax.sharding import PartitionSpec as P

KW = 4
ITERS = 8
CAP = 6


epsilon = 1e-06
highest = lax.Precision.HIGHEST


def own_matvec(matrices, vectors):
    return jnp.sum(matrices * vectors[:, :, None, :], axis=3)


def on_device(
    hidden,
    norm_gain,
    qkv_weight,
    conv_weight,
    conv_state,
    gate_weight,
    prompt_weight,
    ridge_term,
    own_keys,
    own_values,
    prompt_keys,
    prompt_values,
    group_ids,
    lengths,
    out_weight,
):
    gathered = lax.all_gather(hidden, "head", axis=1, tiled=True)
    widened = gathered.astype(jnp.float32)
    scaled = (
        widened
        * lax.rsqrt(jnp.mean(widened * widened, axis=1, keepdims=True) + epsilon)
        * norm_gain
    )
    normed = scaled.astype(jnp.bfloat16)
    row_count, model_width = gathered.shape
    head_count = qkv_weight.shape[1]
    head_size = qkv_weight.shape[3]
    live_rows = [(lengths >= offset).astype(jnp.float32)[:, None, None] for offset in range(KW)]

    def project(part):
        weights = qkv_weight[:, :, part, :].reshape(model_width, head_count * head_size)
        mixing = conv_weight[0, :, part] * jnp.dot(
            normed, weights, preferred_element_type=jnp.float32
        ).reshape(row_count, head_count, head_size)
        for offset in range(1, KW):
            mixing = mixing + conv_weight[offset, :, part] * conv_state[
                :, offset - 1, :, part
            ].astype(jnp.float32) * live_rows[offset]
        return jax.nn.silu(mixing)

    queries = project(0)
    queries = queries * lax.rsqrt(jnp.sum(queries * queries, axis=2, keepdims=True) + epsilon)
    key_now = project(1)
    key_now = key_now * lax.rsqrt(jnp.sum(key_now * key_now, axis=2, keepdims=True) + epsilon)
    value_now = project(2)
    gate_logit = jnp.dot(
        normed, gate_weight.reshape(model_width, 2 * head_count), preferred_element_type=jnp.float32
    ).reshape(row_count, 2, head_count)
    decay_col = jax.nn.sigmoid(gate_logit[:, 0])[:, :, None]
    write_col = jax.nn.sigmoid(gate_logit[:, 1])[:, :, None]
    weight_col = prompt_weight[:, :, None]
    ridge_col = ridge_term[None, :, None]

    peer_count = lax.axis_size("req")
    group_count = prompt_keys.shape[0]
    capacity = CAP
    slot_count = peer_count * capacity
    mask_of_live = lengths > 0
    owner_of = group_ids // group_count
    local_group = group_ids % group_count
    order_ids = jnp.arange(row_count)
    earlier = (
        (order_ids[None, :] < order_ids[:, None])
        & (owner_of[None, :] == owner_of[:, None])
        & mask_of_live[None, :]
    )
    rank_of = jnp.sum(earlier.astype(jnp.int32), axis=1)
    routed = mask_of_live & (rank_of < capacity)
    slot_of = jnp.where(routed, owner_of * capacity + rank_of, 0)
    hits = (slot_of[:, None] == jnp.arange(slot_count)[None, :]) & routed[:, None]
    filled = jnp.any(hits, axis=0)
    source = jnp.sum(jnp.where(hits, order_ids[:, None], 0), axis=0) + jnp.where(
        filled, 0, row_count
    )
    slot_label = jnp.sum(jnp.where(hits, (local_group + 1)[:, None], 0), axis=0)
    source, slot_of, routed, slot_label = lax.optimization_barrier(
        (source, slot_of, routed, slot_label)
    )

    def pack(vectors):
        padded = jnp.concatenate(
            [vectors, jnp.zeros((1,) + vectors.shape[1:], vectors.dtype)], axis=0
        )
        return jnp.take(padded, source, axis=0, mode="clip")

    def exchange(slots):
        shaped = slots.reshape((peer_count, capacity) + slots.shape[1:])
        moved = lax.all_to_all(shaped, "req", split_axis=0, concat_axis=0, tiled=True)
        return moved.reshape(slots.shape)

    def unpack(slots):
        taken = jnp.take(slots, slot_of, axis=0, mode="clip")
        return jnp.where(routed[:, None, None], taken, 0.0)

    def owner_apply(states, incoming, chosen):
        products = jnp.einsum("shj,ghij->gshi", incoming, states, precision=highest)
        total = jnp.where(chosen[0][:, None, None], products[0], 0.0)
        for group in range(1, group_count):
            total = total + jnp.where(chosen[group][:, None, None], products[group], 0.0)
        return total

    def cg_step(arrived, carry):
        solution, residual, direction, norm_now = carry
        shares = unpack(exchange(owner_apply(prompt_keys, arrived, chosen)))
        shared = weight_col * shares + own_matvec(own_keys, direction)
        product = (
            decay_col * shared
            + write_col * key_now * jnp.sum(key_now * direction, axis=2, keepdims=True)
            + ridge_col * direction
        )
        step_size = norm_now / jnp.sum(direction * product, axis=2, keepdims=True)
        solution = solution + step_size * direction
        residual = residual - step_size * product
        norm_next = jnp.sum(residual * residual, axis=2, keepdims=True)
        direction = residual + norm_next / norm_now * direction
        return solution, residual, direction, norm_next

    label_row = jnp.broadcast_to(
        slot_label.astype(jnp.float32)[:, None, None], (slot_count, 1, head_size)
    )
    first = exchange(jnp.concatenate([pack(queries), label_row], axis=1))
    labels_in = first[:, head_count, 0]
    chosen = [labels_in == float(group + 1) for group in range(group_count)]
    chosen = list(lax.optimization_barrier(tuple(chosen)))
    carry = (
        jnp.zeros_like(queries),
        queries,
        queries,
        jnp.sum(queries * queries, axis=2, keepdims=True),
    )
    carry = cg_step(first[:, :head_count], carry)
    carry = lax.fori_loop(
        1, ITERS - 1, lambda _, state: cg_step(exchange(pack(state[2])), state), carry
    )
    solution, residual, direction, norm_now = carry

    both = exchange(jnp.concatenate([pack(direction), pack(solution)], axis=1))
    held = both[:, :head_count]
    owner_out = jnp.concatenate(
        [
            owner_apply(prompt_keys, held, chosen),
            owner_apply(prompt_values, both[:, head_count:], chosen),
            owner_apply(prompt_values, held, chosen),
        ],
        axis=1,
    )
    returned = unpack(exchange(owner_out))
    own_out_partial = own_matvec(own_values, solution)
    own_out_direction = own_matvec(own_values, direction)
    partial = solution
    shares = returned[:, :head_count]
    shared = weight_col * shares + own_matvec(own_keys, direction)
    product = (
        decay_col * shared
        + write_col * key_now * jnp.sum(key_now * direction, axis=2, keepdims=True)
        + ridge_col * direction
    )
    step_last = norm_now / jnp.sum(direction * product, axis=2, keepdims=True)
    solution = partial + step_last * direction
    value_sum = returned[:, head_count : 2 * head_count] + step_last * returned[:, 2 * head_count :]
    own_out = own_out_partial + step_last * own_out_direction
    shared_out = weight_col * value_sum + own_out
    readout = decay_col * shared_out + write_col * value_now * jnp.sum(
        key_now * solution, axis=2, keepdims=True
    )
    normalized = (
        readout * lax.rsqrt(jnp.mean(readout * readout, axis=2, keepdims=True) + epsilon)
    ).astype(jnp.bfloat16)
    partial_value = jnp.dot(
        normalized.reshape(row_count, head_count * head_size),
        out_weight.reshape(head_count * head_size, model_width),
        preferred_element_type=jnp.float32,
    )
    head_peers = lax.axis_size("head")
    if head_peers == 2:
        me = lax.axis_index("head")
        width = model_width // 2
        mine = lax.dynamic_slice_in_dim(partial_value, me * width, width, axis=1)
        theirs = lax.dynamic_slice_in_dim(partial_value, (1 - me) * width, width, axis=1)
        attended = mine + lax.ppermute(theirs, "head", [(0, 1), (1, 0)])
    else:
        attended = lax.psum_scatter(
            partial_value.astype(jnp.bfloat16), "head", scatter_dimension=1, tiled=True
        ).astype(jnp.float32)
    widened_own = hidden.astype(jnp.float32)
    combined = jnp.where(mask_of_live[:, None], widened_own + attended, widened_own)
    return combined.astype(jnp.bfloat16)


def solution(mesh):
    in_specs = (
        P("req", "head"),
        P(),
        P(None, "head", None, None),
        P(None, "head", None, None),
        P("req", None, "head", None, None),
        P(None, None, "head"),
        P("req", "head"),
        P("head"),
        P("req", "head", None, None),
        P("req", "head", None, None),
        P("req", "head", None, None),
        P("req", "head", None, None),
        P("req"),
        P("req"),
        P("head", None, None),
    )
    out_specs = P("req", "head")
    return jax.shard_map(
        on_device, mesh=mesh, in_specs=in_specs, out_specs=out_specs, check_vma=False
    )
```

```python
import jax
import jax.numpy as jnp
from jax import lax
from jax.sharding import PartitionSpec as P

KW = 4
ITERS = 8
CAP = 6


epsilon = 1e-06
highest = lax.Precision.HIGHEST


def own_matvec(matrices, vectors):
    return jnp.sum(matrices * vectors[:, :, None, :], axis=3)


def on_device(
    hidden,
    norm_gain,
    qkv_weight,
    conv_weight,
    conv_state,
    gate_weight,
    prompt_weight,
    ridge_term,
    own_keys,
    own_values,
    prompt_keys,
    prompt_values,
    group_ids,
    lengths,
    out_weight,
):
    gathered = lax.all_gather(hidden, "head", axis=1, tiled=True)
    widened = gathered.astype(jnp.float32)
    scaled = (
        widened
        * lax.rsqrt(jnp.mean(widened * widened, axis=1, keepdims=True) + epsilon)
        * norm_gain
    )
    normed = scaled.astype(jnp.bfloat16)
    row_count, model_width = gathered.shape
    head_count = qkv_weight.shape[1]
    head_size = qkv_weight.shape[3]
    projected = jnp.dot(
        normed,
        qkv_weight.reshape(model_width, head_count * 3 * head_size),
        preferred_element_type=jnp.float32,
    ).reshape(row_count, head_count, 3, head_size)
    mixing = conv_weight[0] * projected
    for offset in range(1, KW):
        usable = (lengths >= offset).astype(jnp.float32)[:, None, None, None]
        mixing = (
            mixing + conv_weight[offset] * conv_state[:, offset - 1].astype(jnp.float32) * usable
        )
    active = jax.nn.silu(mixing)
    queries = active[:, :, 0]
    queries = queries * lax.rsqrt(jnp.sum(queries * queries, axis=2, keepdims=True) + epsilon)
    key_now = active[:, :, 1]
    key_now = key_now * lax.rsqrt(jnp.sum(key_now * key_now, axis=2, keepdims=True) + epsilon)
    value_now = active[:, :, 2]
    gate_logit = jnp.dot(
        normed, gate_weight.reshape(model_width, 2 * head_count), preferred_element_type=jnp.float32
    ).reshape(row_count, 2, head_count)
    decay_col = jax.nn.sigmoid(gate_logit[:, 0])[:, :, None]
    write_col = jax.nn.sigmoid(gate_logit[:, 1])[:, :, None]
    weight_col = prompt_weight[:, :, None]
    ridge_col = ridge_term[None, :, None]

    peer_count = lax.axis_size("req")
    group_count = prompt_keys.shape[0]
    capacity = CAP
    slot_count = peer_count * capacity
    mask_of_live = lengths > 0
    owner_of = group_ids // group_count
    local_group = group_ids % group_count
    order_ids = jnp.arange(row_count)
    earlier = (
        (order_ids[None, :] < order_ids[:, None])
        & (owner_of[None, :] == owner_of[:, None])
        & mask_of_live[None, :]
    )
    rank_of = jnp.sum(earlier.astype(jnp.int32), axis=1)
    routed = mask_of_live & (rank_of < capacity)
    slot_of = jnp.clip(jnp.where(routed, owner_of * capacity + rank_of, 0), 0, slot_count - 1)
    hits = (slot_of[:, None] == jnp.arange(slot_count)[None, :]) & routed[:, None]
    filled = jnp.any(hits, axis=0)
    source = jnp.sum(jnp.where(hits, order_ids[:, None], 0), axis=0) + jnp.where(
        filled, 0, row_count
    )
    slot_label = jnp.sum(jnp.where(hits, (local_group + 1)[:, None], 0), axis=0)

    def pack(vectors):
        padded = jnp.concatenate(
            [vectors, jnp.zeros((1,) + vectors.shape[1:], vectors.dtype)], axis=0
        )
        return padded.at[source].get(mode="promise_in_bounds")

    def exchange(slots):
        shaped = slots.reshape((peer_count, capacity) + slots.shape[1:])
        moved = lax.all_to_all(shaped, "req", split_axis=0, concat_axis=0, tiled=True)
        return moved.reshape(slots.shape)

    def unpack(slots):
        taken = slots.at[slot_of].get(mode="promise_in_bounds")
        return jnp.where(routed[:, None, None], taken, 0.0)

    def owner_apply(states, incoming, chosen):
        products = jnp.einsum("shj,ghij->gshi", incoming, states, precision=highest)
        total = jnp.where(chosen[0][:, None, None], products[0], 0.0)
        for group in range(1, group_count):
            total = total + jnp.where(chosen[group][:, None, None], products[group], 0.0)
        return total

    def cg_step(arrived, carry):
        solution, residual, direction, norm_now = carry
        shares = unpack(exchange(owner_apply(prompt_keys, arrived, chosen)))
        shared = weight_col * shares + own_matvec(own_keys, direction)
        product = (
            decay_col * shared
            + write_col * key_now * jnp.sum(key_now * direction, axis=2, keepdims=True)
            + ridge_col * direction
        )
        step_size = norm_now / jnp.sum(direction * product, axis=2, keepdims=True)
        solution = solution + step_size * direction
        residual = residual - step_size * product
        norm_next = jnp.sum(residual * residual, axis=2, keepdims=True)
        direction = residual + norm_next / norm_now * direction
        return solution, residual, direction, norm_next

    label_row = jnp.broadcast_to(
        slot_label.astype(jnp.float32)[:, None, None], (slot_count, 1, head_size)
    )
    first = exchange(jnp.concatenate([pack(queries), label_row], axis=1))
    labels_in = first[:, head_count, 0]
    chosen = [labels_in == float(group + 1) for group in range(group_count)]
    carry = (
        jnp.zeros_like(queries),
        queries,
        queries,
        jnp.sum(queries * queries, axis=2, keepdims=True),
    )
    carry = cg_step(first[:, :head_count], carry)
    carry = lax.fori_loop(
        1, ITERS - 1, lambda _, state: cg_step(exchange(pack(state[2])), state), carry
    )
    solution, residual, direction, norm_now = carry

    both = exchange(jnp.concatenate([pack(direction), pack(solution)], axis=1))
    held = both[:, :head_count]
    owner_out = jnp.concatenate(
        [
            owner_apply(prompt_keys, held, chosen),
            owner_apply(prompt_values, both[:, head_count:], chosen),
            owner_apply(prompt_values, held, chosen),
        ],
        axis=1,
    )
    returned = unpack(exchange(owner_out))
    own_out_partial = own_matvec(own_values, solution)
    own_out_direction = own_matvec(own_values, direction)
    partial = solution
    shares = returned[:, :head_count]
    shared = weight_col * shares + own_matvec(own_keys, direction)
    product = (
        decay_col * shared
        + write_col * key_now * jnp.sum(key_now * direction, axis=2, keepdims=True)
        + ridge_col * direction
    )
    step_last = norm_now / jnp.sum(direction * product, axis=2, keepdims=True)
    solution = partial + step_last * direction
    value_sum = returned[:, head_count : 2 * head_count] + step_last * returned[:, 2 * head_count :]
    own_out = own_out_partial + step_last * own_out_direction
    shared_out = weight_col * value_sum + own_out
    readout = decay_col * shared_out + write_col * value_now * jnp.sum(
        key_now * solution, axis=2, keepdims=True
    )
    normalized = (
        readout * lax.rsqrt(jnp.mean(readout * readout, axis=2, keepdims=True) + epsilon)
    ).astype(jnp.bfloat16)
    partial_value = jnp.dot(
        normalized.reshape(row_count, head_count * head_size),
        out_weight.reshape(head_count * head_size, model_width),
        preferred_element_type=jnp.float32,
    )
    head_peers = lax.axis_size("head")
    if head_peers == 2:
        me = lax.axis_index("head")
        width = model_width // 2
        mine = lax.dynamic_slice_in_dim(partial_value, me * width, width, axis=1)
        theirs = lax.dynamic_slice_in_dim(partial_value, (1 - me) * width, width, axis=1)
        attended = mine + lax.ppermute(theirs, "head", [(0, 1), (1, 0)])
    else:
        attended = lax.psum_scatter(
            partial_value.astype(jnp.bfloat16), "head", scatter_dimension=1, tiled=True
        ).astype(jnp.float32)
    widened_own = hidden.astype(jnp.float32)
    combined = jnp.where(mask_of_live[:, None], widened_own + attended, widened_own)
    return combined.astype(jnp.bfloat16)


def solution(mesh):
    in_specs = (
        P("req", "head"),
        P(),
        P(None, "head", None, None),
        P(None, "head", None, None),
        P("req", None, "head", None, None),
        P(None, None, "head"),
        P("req", "head"),
        P("head"),
        P("req", "head", None, None),
        P("req", "head", None, None),
        P("req", "head", None, None),
        P("req", "head", None, None),
        P("req"),
        P("req"),
        P("head", None, None),
    )
    out_specs = P("req", "head")
    return jax.shard_map(
        on_device, mesh=mesh, in_specs=in_specs, out_specs=out_specs, check_vma=False
    )
```

```python
import jax
import jax.numpy as jnp
from jax import lax
from jax.sharding import PartitionSpec as P

KW = 4
ITERS = 8
CAP = 6


epsilon = 1e-06
highest = lax.Precision.HIGHEST


def own_matvec(matrices, vectors):
    return jnp.sum(matrices * vectors[:, :, None, :], axis=3)


def on_device(
    hidden,
    norm_gain,
    qkv_weight,
    conv_weight,
    conv_state,
    gate_weight,
    prompt_weight,
    ridge_term,
    own_keys,
    own_values,
    prompt_keys,
    prompt_values,
    group_ids,
    lengths,
    out_weight,
):
    if lax.axis_size("head") == 2:
        other_half = lax.ppermute(hidden, "head", [(0, 1), (1, 0)])
        first_core = lax.axis_index("head") == 0
        gathered = jnp.where(
            first_core,
            jnp.concatenate([hidden, other_half], axis=1),
            jnp.concatenate([other_half, hidden], axis=1),
        )
    else:
        gathered = lax.all_gather(hidden, "head", axis=1, tiled=True)
    widened = gathered.astype(jnp.float32)
    scaled = (
        widened
        * lax.rsqrt(jnp.mean(widened * widened, axis=1, keepdims=True) + epsilon)
        * norm_gain
    )
    normed = scaled.astype(jnp.bfloat16)
    row_count, model_width = gathered.shape
    head_count = qkv_weight.shape[1]
    head_size = qkv_weight.shape[3]
    projected = jnp.dot(
        normed,
        qkv_weight.reshape(model_width, head_count * 3 * head_size),
        preferred_element_type=jnp.float32,
    ).reshape(row_count, head_count, 3, head_size)
    mixing = conv_weight[0] * projected
    for offset in range(1, KW):
        usable = (lengths >= offset).astype(jnp.float32)[:, None, None, None]
        mixing = (
            mixing + conv_weight[offset] * conv_state[:, offset - 1].astype(jnp.float32) * usable
        )
    active = jax.nn.silu(mixing)
    queries = active[:, :, 0]
    queries = queries * lax.rsqrt(jnp.sum(queries * queries, axis=2, keepdims=True) + epsilon)
    key_now = active[:, :, 1]
    key_now = key_now * lax.rsqrt(jnp.sum(key_now * key_now, axis=2, keepdims=True) + epsilon)
    value_now = active[:, :, 2]
    gate_logit = jnp.dot(
        normed, gate_weight.reshape(model_width, 2 * head_count), preferred_element_type=jnp.float32
    ).reshape(row_count, 2, head_count)
    decay_col = jax.nn.sigmoid(gate_logit[:, 0])[:, :, None]
    write_col = jax.nn.sigmoid(gate_logit[:, 1])[:, :, None]
    weight_col = prompt_weight[:, :, None]
    ridge_col = ridge_term[None, :, None]

    peer_count = lax.axis_size("req")
    group_count = prompt_keys.shape[0]
    capacity = CAP
    slot_count = peer_count * capacity
    mask_of_live = lengths > 0
    owner_of = group_ids // group_count
    local_group = group_ids % group_count
    order_ids = jnp.arange(row_count)
    earlier = (
        (order_ids[None, :] < order_ids[:, None])
        & (owner_of[None, :] == owner_of[:, None])
        & mask_of_live[None, :]
    )
    rank_of = jnp.sum(earlier.astype(jnp.int32), axis=1)
    routed = mask_of_live & (rank_of < capacity)
    slot_of = jnp.where(routed, owner_of * capacity + rank_of, 0)
    hits = (slot_of[:, None] == jnp.arange(slot_count)[None, :]) & routed[:, None]
    filled = jnp.any(hits, axis=0)
    source = jnp.sum(jnp.where(hits, order_ids[:, None], 0), axis=0) + jnp.where(
        filled, 0, row_count
    )
    slot_label = jnp.sum(jnp.where(hits, (local_group + 1)[:, None], 0), axis=0)

    def pack(vectors):
        padded = jnp.concatenate(
            [vectors, jnp.zeros((1,) + vectors.shape[1:], vectors.dtype)], axis=0
        )
        return jnp.take(padded, source, axis=0, mode="clip")

    def exchange(slots):
        shaped = slots.reshape((peer_count, capacity) + slots.shape[1:])
        moved = lax.all_to_all(shaped, "req", split_axis=0, concat_axis=0, tiled=True)
        return moved.reshape(slots.shape)

    def unpack(slots):
        taken = jnp.take(slots, slot_of, axis=0, mode="clip")
        return jnp.where(routed[:, None, None], taken, 0.0)

    def owner_apply(states, incoming, chosen):
        products = jnp.einsum("shj,ghij->gshi", incoming, states, precision=highest)
        total = jnp.where(chosen[0][:, None, None], products[0], 0.0)
        for group in range(1, group_count):
            total = total + jnp.where(chosen[group][:, None, None], products[group], 0.0)
        return total

    def cg_step(arrived, carry):
        solution, residual, direction, norm_now = carry
        shares = unpack(exchange(owner_apply(prompt_keys, arrived, chosen)))
        shared = weight_col * shares + own_matvec(own_keys, direction)
        product = (
            decay_col * shared
            + write_col * key_now * jnp.sum(key_now * direction, axis=2, keepdims=True)
            + ridge_col * direction
        )
        step_size = norm_now / jnp.sum(direction * product, axis=2, keepdims=True)
        solution = solution + step_size * direction
        residual = residual - step_size * product
        norm_next = jnp.sum(residual * residual, axis=2, keepdims=True)
        direction = residual + norm_next / norm_now * direction
        return solution, residual, direction, norm_next

    label_row = jnp.broadcast_to(
        slot_label.astype(jnp.float32)[:, None, None], (slot_count, 1, head_size)
    )
    first = exchange(jnp.concatenate([pack(queries), label_row], axis=1))
    labels_in = first[:, head_count, 0]
    chosen = [labels_in == float(group + 1) for group in range(group_count)]
    carry = (
        jnp.zeros_like(queries),
        queries,
        queries,
        jnp.sum(queries * queries, axis=2, keepdims=True),
    )
    carry = cg_step(first[:, :head_count], carry)
    carry = lax.fori_loop(
        1, ITERS - 1, lambda _, state: cg_step(exchange(pack(state[2])), state), carry
    )
    solution, residual, direction, norm_now = carry

    both = exchange(jnp.concatenate([pack(direction), pack(solution)], axis=1))
    held = both[:, :head_count]
    owner_out = jnp.concatenate(
        [
            owner_apply(prompt_keys, held, chosen),
            owner_apply(prompt_values, both[:, head_count:], chosen),
            owner_apply(prompt_values, held, chosen),
        ],
        axis=1,
    )
    returned = unpack(exchange(owner_out))
    own_out_partial = own_matvec(own_values, solution)
    own_out_direction = own_matvec(own_values, direction)
    partial = solution
    shares = returned[:, :head_count]
    shared = weight_col * shares + own_matvec(own_keys, direction)
    product = (
        decay_col * shared
        + write_col * key_now * jnp.sum(key_now * direction, axis=2, keepdims=True)
        + ridge_col * direction
    )
    step_last = norm_now / jnp.sum(direction * product, axis=2, keepdims=True)
    solution = partial + step_last * direction
    value_sum = returned[:, head_count : 2 * head_count] + step_last * returned[:, 2 * head_count :]
    own_out = own_out_partial + step_last * own_out_direction
    shared_out = weight_col * value_sum + own_out
    readout = decay_col * shared_out + write_col * value_now * jnp.sum(
        key_now * solution, axis=2, keepdims=True
    )
    normalized = (
        readout * lax.rsqrt(jnp.mean(readout * readout, axis=2, keepdims=True) + epsilon)
    ).astype(jnp.bfloat16)
    partial_value = jnp.dot(
        normalized.reshape(row_count, head_count * head_size),
        out_weight.reshape(head_count * head_size, model_width),
        preferred_element_type=jnp.float32,
    )
    head_peers = lax.axis_size("head")
    if head_peers == 2:
        me = lax.axis_index("head")
        width = model_width // 2
        mine = lax.dynamic_slice_in_dim(partial_value, me * width, width, axis=1)
        theirs = lax.dynamic_slice_in_dim(partial_value, (1 - me) * width, width, axis=1)
        attended = mine + lax.ppermute(theirs, "head", [(0, 1), (1, 0)])
    else:
        attended = lax.psum_scatter(
            partial_value.astype(jnp.bfloat16), "head", scatter_dimension=1, tiled=True
        ).astype(jnp.float32)
    widened_own = hidden.astype(jnp.float32)
    combined = jnp.where(mask_of_live[:, None], widened_own + attended, widened_own)
    return combined.astype(jnp.bfloat16)


def solution(mesh):
    in_specs = (
        P("req", "head"),
        P(),
        P(None, "head", None, None),
        P(None, "head", None, None),
        P("req", None, "head", None, None),
        P(None, None, "head"),
        P("req", "head"),
        P("head"),
        P("req", "head", None, None),
        P("req", "head", None, None),
        P("req", "head", None, None),
        P("req", "head", None, None),
        P("req"),
        P("req"),
        P("head", None, None),
    )
    out_specs = P("req", "head")
    return jax.shard_map(
        on_device, mesh=mesh, in_specs=in_specs, out_specs=out_specs, check_vma=False
    )
```

```python
import jax
import jax.numpy as jnp
from jax import lax
from jax.sharding import PartitionSpec as P

KW = 4
ITERS = 8
CAP = 6


epsilon = 1e-06
highest = lax.Precision.HIGHEST


def own_matvec(matrices, vectors):
    return jnp.sum(matrices * vectors[:, :, None, :], axis=3)


def on_device(
    hidden,
    norm_gain,
    qkv_weight,
    conv_weight,
    conv_state,
    gate_weight,
    prompt_weight,
    ridge_term,
    own_keys,
    own_values,
    prompt_keys,
    prompt_values,
    group_ids,
    lengths,
    out_weight,
):
    if lax.axis_size("head") == 2:
        other_half = lax.ppermute(hidden, "head", [(0, 1), (1, 0)])
        first_core = lax.axis_index("head") == 0
        gathered = jnp.where(
            first_core,
            jnp.concatenate([hidden, other_half], axis=1),
            jnp.concatenate([other_half, hidden], axis=1),
        )
    else:
        gathered = lax.all_gather(hidden, "head", axis=1, tiled=True)
    widened = gathered.astype(jnp.float32)
    scaled = (
        widened
        * lax.rsqrt(jnp.mean(widened * widened, axis=1, keepdims=True) + epsilon)
        * norm_gain
    )
    normed = scaled.astype(jnp.bfloat16)
    row_count, model_width = gathered.shape
    head_count = qkv_weight.shape[1]
    head_size = qkv_weight.shape[3]
    projected = jnp.dot(
        normed,
        qkv_weight.reshape(model_width, head_count * 3 * head_size),
        preferred_element_type=jnp.float32,
    ).reshape(row_count, head_count, 3, head_size)
    mixing = conv_weight[0] * projected
    for offset in range(1, KW):
        usable = (lengths >= offset).astype(jnp.float32)[:, None, None, None]
        mixing = (
            mixing + conv_weight[offset] * conv_state[:, offset - 1].astype(jnp.float32) * usable
        )
    active = jax.nn.silu(mixing)
    queries = active[:, :, 0]
    queries = queries * lax.rsqrt(jnp.sum(queries * queries, axis=2, keepdims=True) + epsilon)
    key_now = active[:, :, 1]
    key_now = key_now * lax.rsqrt(jnp.sum(key_now * key_now, axis=2, keepdims=True) + epsilon)
    value_now = active[:, :, 2]
    gate_logit = jnp.dot(
        normed, gate_weight.reshape(model_width, 2 * head_count), preferred_element_type=jnp.float32
    ).reshape(row_count, 2, head_count)
    decay_col = jax.nn.sigmoid(gate_logit[:, 0])[:, :, None]
    write_col = jax.nn.sigmoid(gate_logit[:, 1])[:, :, None]
    weight_col = prompt_weight[:, :, None]
    ridge_col = ridge_term[None, :, None]

    peer_count = lax.axis_size("req")
    group_count = prompt_keys.shape[0]
    capacity = CAP
    slot_count = peer_count * capacity
    mask_of_live = lengths > 0
    owner_of = group_ids // group_count
    local_group = group_ids % group_count
    order_ids = jnp.arange(row_count)
    earlier = (
        (order_ids[None, :] < order_ids[:, None])
        & (owner_of[None, :] == owner_of[:, None])
        & mask_of_live[None, :]
    )
    rank_of = jnp.sum(earlier.astype(jnp.int32), axis=1)
    routed = mask_of_live & (rank_of < capacity)
    slot_of = jnp.where(routed, owner_of * capacity + rank_of, 0)
    hits = (slot_of[:, None] == jnp.arange(slot_count)[None, :]) & routed[:, None]
    filled = jnp.any(hits, axis=0)
    source = jnp.sum(jnp.where(hits, order_ids[:, None], 0), axis=0) + jnp.where(
        filled, 0, row_count
    )
    slot_label = jnp.sum(jnp.where(hits, (local_group + 1)[:, None], 0), axis=0)

    def pack(vectors):
        padded = jnp.concatenate(
            [vectors, jnp.zeros((1,) + vectors.shape[1:], vectors.dtype)], axis=0
        )
        return jnp.take(padded, source, axis=0, mode="clip")

    def exchange(slots):
        shaped = slots.reshape((peer_count, capacity) + slots.shape[1:])
        moved = lax.all_to_all(shaped, "req", split_axis=0, concat_axis=0, tiled=True)
        return moved.reshape(slots.shape)

    def unpack(slots):
        taken = jnp.take(slots, slot_of, axis=0, mode="clip")
        return jnp.where(routed[:, None, None], taken, 0.0)

    def owner_apply(states, incoming, chosen):
        products = jnp.einsum("shj,ghij->gshi", incoming, states, precision=highest)
        total = jnp.where(chosen[0][:, None, None], products[0], 0.0)
        for group in range(1, group_count):
            total = total + jnp.where(chosen[group][:, None, None], products[group], 0.0)
        return total

    def cg_step(arrived, carry):
        solution, residual, direction, norm_now = carry
        shares = unpack(exchange(owner_apply(prompt_keys, arrived, chosen)))
        shared = weight_col * shares + own_matvec(own_keys, direction)
        product = (
            decay_col * shared
            + write_col * key_now * jnp.sum(key_now * direction, axis=2, keepdims=True)
            + ridge_col * direction
        )
        step_size = norm_now / jnp.sum(direction * product, axis=2, keepdims=True)
        solution = solution + step_size * direction
        residual = residual - step_size * product
        norm_next = jnp.sum(residual * residual, axis=2, keepdims=True)
        direction = residual + norm_next / norm_now * direction
        return solution, residual, direction, norm_next

    label_row = jnp.broadcast_to(
        slot_label.astype(jnp.float32)[:, None, None], (slot_count, 1, head_size)
    )
    first = exchange(jnp.concatenate([pack(queries), label_row], axis=1))
    labels_in = first[:, head_count, 0]
    chosen = [labels_in == float(group + 1) for group in range(group_count)]
    carry = (
        jnp.zeros_like(queries),
        queries,
        queries,
        jnp.sum(queries * queries, axis=2, keepdims=True),
    )
    carry = cg_step(first[:, :head_count], carry)
    carry = lax.fori_loop(
        1, ITERS - 1, lambda _, state: cg_step(exchange(pack(state[2])), state), carry
    )
    solution, residual, direction, norm_now = carry

    both = exchange(
        jnp.concatenate([pack(direction), pack(solution)], axis=1).astype(jnp.bfloat16)
    ).astype(jnp.float32)
    held = both[:, :head_count]
    owner_out = jnp.concatenate(
        [
            owner_apply(prompt_keys, held, chosen),
            owner_apply(prompt_values, both[:, head_count:], chosen),
            owner_apply(prompt_values, held, chosen),
        ],
        axis=1,
    )
    returned = unpack(exchange(owner_out.astype(jnp.bfloat16)).astype(jnp.float32))
    own_out_partial = own_matvec(own_values, solution)
    own_out_direction = own_matvec(own_values, direction)
    partial = solution
    shares = returned[:, :head_count]
    shared = weight_col * shares + own_matvec(own_keys, direction)
    product = (
        decay_col * shared
        + write_col * key_now * jnp.sum(key_now * direction, axis=2, keepdims=True)
        + ridge_col * direction
    )
    step_last = norm_now / jnp.sum(direction * product, axis=2, keepdims=True)
    solution = partial + step_last * direction
    value_sum = returned[:, head_count : 2 * head_count] + step_last * returned[:, 2 * head_count :]
    own_out = own_out_partial + step_last * own_out_direction
    shared_out = weight_col * value_sum + own_out
    readout = decay_col * shared_out + write_col * value_now * jnp.sum(
        key_now * solution, axis=2, keepdims=True
    )
    normalized = (
        readout * lax.rsqrt(jnp.mean(readout * readout, axis=2, keepdims=True) + epsilon)
    ).astype(jnp.bfloat16)
    partial_value = jnp.dot(
        normalized.reshape(row_count, head_count * head_size),
        out_weight.reshape(head_count * head_size, model_width),
        preferred_element_type=jnp.float32,
    )
    head_peers = lax.axis_size("head")
    if head_peers == 2:
        me = lax.axis_index("head")
        width = model_width // 2
        mine = lax.dynamic_slice_in_dim(partial_value, me * width, width, axis=1)
        theirs = lax.dynamic_slice_in_dim(partial_value, (1 - me) * width, width, axis=1)
        attended = mine + lax.ppermute(theirs, "head", [(0, 1), (1, 0)])
    else:
        attended = lax.psum_scatter(
            partial_value.astype(jnp.bfloat16), "head", scatter_dimension=1, tiled=True
        ).astype(jnp.float32)
    widened_own = hidden.astype(jnp.float32)
    combined = jnp.where(mask_of_live[:, None], widened_own + attended, widened_own)
    return combined.astype(jnp.bfloat16)


def solution(mesh):
    in_specs = (
        P("req", "head"),
        P(),
        P(None, "head", None, None),
        P(None, "head", None, None),
        P("req", None, "head", None, None),
        P(None, None, "head"),
        P("req", "head"),
        P("head"),
        P("req", "head", None, None),
        P("req", "head", None, None),
        P("req", "head", None, None),
        P("req", "head", None, None),
        P("req"),
        P("req"),
        P("head", None, None),
    )
    out_specs = P("req", "head")
    return jax.shard_map(
        on_device, mesh=mesh, in_specs=in_specs, out_specs=out_specs, check_vma=False
    )
```

```python
import jax
import jax.numpy as jnp
from jax import lax
from jax.sharding import PartitionSpec as P

KW = 4
ITERS = 8
CAP = 6


epsilon = 1e-06
highest = lax.Precision.HIGHEST


def own_matvec(matrices, vectors):
    return jnp.sum(matrices * vectors[:, :, None, :], axis=3)


def on_device(
    hidden,
    norm_gain,
    qkv_weight,
    conv_weight,
    conv_state,
    gate_weight,
    prompt_weight,
    ridge_term,
    own_keys,
    own_values,
    prompt_keys,
    prompt_values,
    group_ids,
    lengths,
    out_weight,
):
    if lax.axis_size("head") == 2:
        other_half = lax.ppermute(hidden, "head", [(0, 1), (1, 0)])
        first_core = lax.axis_index("head") == 0
        gathered = jnp.where(
            first_core,
            jnp.concatenate([hidden, other_half], axis=1),
            jnp.concatenate([other_half, hidden], axis=1),
        )
    else:
        gathered = lax.all_gather(hidden, "head", axis=1, tiled=True)
    widened = gathered.astype(jnp.float32)
    scaled = (
        widened
        * lax.rsqrt(jnp.mean(widened * widened, axis=1, keepdims=True) + epsilon)
        * norm_gain
    )
    normed = scaled.astype(jnp.bfloat16)
    row_count, model_width = gathered.shape
    head_count = qkv_weight.shape[1]
    head_size = qkv_weight.shape[3]
    projected = jnp.dot(
        normed,
        qkv_weight.reshape(model_width, head_count * 3 * head_size),
        preferred_element_type=jnp.float32,
    ).reshape(row_count, head_count, 3, head_size)
    mixing = conv_weight[0] * projected
    for offset in range(1, KW):
        usable = (lengths >= offset).astype(jnp.float32)[:, None, None, None]
        mixing = (
            mixing + conv_weight[offset] * conv_state[:, offset - 1].astype(jnp.float32) * usable
        )
    active = jax.nn.silu(mixing)
    queries = active[:, :, 0]
    queries = queries * lax.rsqrt(jnp.sum(queries * queries, axis=2, keepdims=True) + epsilon)
    key_now = active[:, :, 1]
    key_now = key_now * lax.rsqrt(jnp.sum(key_now * key_now, axis=2, keepdims=True) + epsilon)
    value_now = active[:, :, 2]
    gate_logit = jnp.dot(
        normed, gate_weight.reshape(model_width, 2 * head_count), preferred_element_type=jnp.float32
    ).reshape(row_count, 2, head_count)
    decay_col = jax.nn.sigmoid(gate_logit[:, 0])[:, :, None]
    write_col = jax.nn.sigmoid(gate_logit[:, 1])[:, :, None]
    weight_col = prompt_weight[:, :, None]
    ridge_col = ridge_term[None, :, None]
    lane_shape = (row_count, head_count, head_size)
    decay_b = jnp.broadcast_to(decay_col, lane_shape)
    write_b = jnp.broadcast_to(write_col, lane_shape)
    weight_b = jnp.broadcast_to(weight_col, lane_shape)
    ridge_b = jnp.broadcast_to(ridge_col, lane_shape)

    def lane_sum(values):
        return jnp.broadcast_to(jnp.sum(values, axis=2, keepdims=True), values.shape)

    peer_count = lax.axis_size("req")
    group_count = prompt_keys.shape[0]
    capacity = CAP
    slot_count = peer_count * capacity
    mask_of_live = lengths > 0
    owner_of = group_ids // group_count
    local_group = group_ids % group_count
    order_ids = jnp.arange(row_count)
    earlier = (
        (order_ids[None, :] < order_ids[:, None])
        & (owner_of[None, :] == owner_of[:, None])
        & mask_of_live[None, :]
    )
    rank_of = jnp.sum(earlier.astype(jnp.int32), axis=1)
    routed = mask_of_live & (rank_of < capacity)
    slot_of = jnp.where(routed, owner_of * capacity + rank_of, 0)
    hits = (slot_of[:, None] == jnp.arange(slot_count)[None, :]) & routed[:, None]
    filled = jnp.any(hits, axis=0)
    source = jnp.sum(jnp.where(hits, order_ids[:, None], 0), axis=0) + jnp.where(
        filled, 0, row_count
    )
    slot_label = jnp.sum(jnp.where(hits, (local_group + 1)[:, None], 0), axis=0)

    def pack(vectors):
        padded = jnp.concatenate(
            [vectors, jnp.zeros((1,) + vectors.shape[1:], vectors.dtype)], axis=0
        )
        return jnp.take(padded, source, axis=0, mode="clip")

    def exchange(slots):
        shaped = slots.reshape((peer_count, capacity) + slots.shape[1:])
        moved = lax.all_to_all(shaped, "req", split_axis=0, concat_axis=0, tiled=True)
        return moved.reshape(slots.shape)

    def unpack(slots):
        taken = jnp.take(slots, slot_of, axis=0, mode="clip")
        return jnp.where(routed[:, None, None], taken, 0.0)

    def owner_apply(states, incoming, chosen):
        products = jnp.einsum("shj,ghij->gshi", incoming, states, precision=highest)
        total = jnp.where(chosen[0][:, None, None], products[0], 0.0)
        for group in range(1, group_count):
            total = total + jnp.where(chosen[group][:, None, None], products[group], 0.0)
        return total

    def cg_step(arrived, carry):
        solution, residual, direction, norm_now = carry
        shares = unpack(exchange(owner_apply(prompt_keys, arrived, chosen)))
        shared = weight_b * shares + own_matvec(own_keys, direction)
        product = (
            decay_b * shared
            + write_b * key_now * lane_sum(key_now * direction)
            + ridge_b * direction
        )
        step_size = norm_now / lane_sum(direction * product)
        solution = solution + step_size * direction
        residual = residual - step_size * product
        norm_next = lane_sum(residual * residual)
        direction = residual + norm_next / norm_now * direction
        return solution, residual, direction, norm_next

    label_row = jnp.broadcast_to(
        slot_label.astype(jnp.float32)[:, None, None], (slot_count, 1, head_size)
    )
    first = exchange(jnp.concatenate([pack(queries), label_row], axis=1))
    labels_in = first[:, head_count, 0]
    chosen = [labels_in == float(group + 1) for group in range(group_count)]
    carry = (
        jnp.zeros_like(queries),
        queries,
        queries,
        lane_sum(queries * queries),
    )
    carry = cg_step(first[:, :head_count], carry)
    carry = lax.fori_loop(
        1, ITERS - 1, lambda _, state: cg_step(exchange(pack(state[2])), state), carry
    )
    solution, residual, direction, norm_now = carry

    both = exchange(jnp.concatenate([pack(direction), pack(solution)], axis=1))
    held = both[:, :head_count]
    owner_out = jnp.concatenate(
        [
            owner_apply(prompt_keys, held, chosen),
            owner_apply(prompt_values, both[:, head_count:], chosen),
            owner_apply(prompt_values, held, chosen),
        ],
        axis=1,
    )
    returned = unpack(exchange(owner_out))
    own_out_partial = own_matvec(own_values, solution)
    own_out_direction = own_matvec(own_values, direction)
    partial = solution
    shares = returned[:, :head_count]
    shared = weight_b * shares + own_matvec(own_keys, direction)
    product = (
        decay_b * shared
        + write_b * key_now * lane_sum(key_now * direction)
        + ridge_b * direction
    )
    step_last = norm_now / lane_sum(direction * product)
    solution = partial + step_last * direction
    value_sum = returned[:, head_count : 2 * head_count] + step_last * returned[:, 2 * head_count :]
    own_out = own_out_partial + step_last * own_out_direction
    shared_out = weight_col * value_sum + own_out
    readout = decay_col * shared_out + write_col * value_now * jnp.sum(
        key_now * solution, axis=2, keepdims=True
    )
    normalized = (
        readout * lax.rsqrt(jnp.mean(readout * readout, axis=2, keepdims=True) + epsilon)
    ).astype(jnp.bfloat16)
    partial_value = jnp.dot(
        normalized.reshape(row_count, head_count * head_size),
        out_weight.reshape(head_count * head_size, model_width),
        preferred_element_type=jnp.float32,
    )
    head_peers = lax.axis_size("head")
    if head_peers == 2:
        me = lax.axis_index("head")
        width = model_width // 2
        mine = lax.dynamic_slice_in_dim(partial_value, me * width, width, axis=1)
        theirs = lax.dynamic_slice_in_dim(partial_value, (1 - me) * width, width, axis=1)
        attended = mine + lax.ppermute(theirs, "head", [(0, 1), (1, 0)])
    else:
        attended = lax.psum_scatter(
            partial_value.astype(jnp.bfloat16), "head", scatter_dimension=1, tiled=True
        ).astype(jnp.float32)
    widened_own = hidden.astype(jnp.float32)
    combined = jnp.where(mask_of_live[:, None], widened_own + attended, widened_own)
    return combined.astype(jnp.bfloat16)


def solution(mesh):
    in_specs = (
        P("req", "head"),
        P(),
        P(None, "head", None, None),
        P(None, "head", None, None),
        P("req", None, "head", None, None),
        P(None, None, "head"),
        P("req", "head"),
        P("head"),
        P("req", "head", None, None),
        P("req", "head", None, None),
        P("req", "head", None, None),
        P("req", "head", None, None),
        P("req"),
        P("req"),
        P("head", None, None),
    )
    out_specs = P("req", "head")
    return jax.shard_map(
        on_device, mesh=mesh, in_specs=in_specs, out_specs=out_specs, check_vma=False
    )
```

```python
import jax
import jax.numpy as jnp
from jax import lax
from jax.sharding import PartitionSpec as P

KW = 4
ITERS = 8
CAP = 6


epsilon = 1e-06
highest = lax.Precision.HIGHEST


def own_matvec(matrices, vectors):
    return jnp.sum(matrices * vectors[:, :, None, :], axis=3)


def on_device(
    hidden,
    norm_gain,
    qkv_weight,
    conv_weight,
    conv_state,
    gate_weight,
    prompt_weight,
    ridge_term,
    own_keys,
    own_values,
    prompt_keys,
    prompt_values,
    group_ids,
    lengths,
    out_weight,
):
    if lax.axis_size("head") == 2:
        other_half = lax.ppermute(hidden, "head", [(0, 1), (1, 0)])
        first_core = lax.axis_index("head") == 0
        gathered = jnp.where(
            first_core,
            jnp.concatenate([hidden, other_half], axis=1),
            jnp.concatenate([other_half, hidden], axis=1),
        )
    else:
        gathered = lax.all_gather(hidden, "head", axis=1, tiled=True)
    widened = gathered.astype(jnp.float32)
    scaled = (
        widened
        * lax.rsqrt(jnp.mean(widened * widened, axis=1, keepdims=True) + epsilon)
        * norm_gain
    )
    normed = scaled.astype(jnp.bfloat16)
    row_count, model_width = gathered.shape
    head_count = qkv_weight.shape[1]
    head_size = qkv_weight.shape[3]
    projected = jnp.dot(
        normed,
        qkv_weight.reshape(model_width, head_count * 3 * head_size),
        preferred_element_type=jnp.float32,
    ).reshape(row_count, head_count, 3, head_size)
    mixing = conv_weight[0] * projected
    for offset in range(1, KW):
        usable = (lengths >= offset).astype(jnp.float32)[:, None, None, None]
        mixing = (
            mixing + conv_weight[offset] * conv_state[:, offset - 1].astype(jnp.float32) * usable
        )
    active = jax.nn.silu(mixing)
    queries = active[:, :, 0]
    queries = queries * lax.rsqrt(jnp.sum(queries * queries, axis=2, keepdims=True) + epsilon)
    key_now = active[:, :, 1]
    key_now = key_now * lax.rsqrt(jnp.sum(key_now * key_now, axis=2, keepdims=True) + epsilon)
    value_now = active[:, :, 2]
    gate_logit = jnp.dot(
        normed, gate_weight.reshape(model_width, 2 * head_count), preferred_element_type=jnp.float32
    ).reshape(row_count, 2, head_count)
    decay_col = jax.nn.sigmoid(gate_logit[:, 0])[:, :, None]
    write_col = jax.nn.sigmoid(gate_logit[:, 1])[:, :, None]
    weight_col = prompt_weight[:, :, None]
    ridge_col = ridge_term[None, :, None]
    lane_shape = (row_count, head_count, head_size)
    decay_b = jnp.broadcast_to(decay_col, lane_shape)
    write_b = jnp.broadcast_to(write_col, lane_shape)
    weight_b = jnp.broadcast_to(weight_col, lane_shape)
    ridge_b = jnp.broadcast_to(ridge_col, lane_shape)

    def lane_sum(values):
        return jnp.broadcast_to(jnp.sum(values, axis=2, keepdims=True), values.shape)

    peer_count = lax.axis_size("req")
    group_count = prompt_keys.shape[0]
    capacity = CAP
    slot_count = peer_count * capacity
    mask_of_live = lengths > 0
    owner_of = group_ids // group_count
    local_group = group_ids % group_count
    order_ids = jnp.arange(row_count)
    earlier = (
        (order_ids[None, :] < order_ids[:, None])
        & (owner_of[None, :] == owner_of[:, None])
        & mask_of_live[None, :]
    )
    rank_of = jnp.sum(earlier.astype(jnp.int32), axis=1)
    routed = mask_of_live & (rank_of < capacity)
    slot_of = jnp.where(routed, owner_of * capacity + rank_of, 0)
    hits = (slot_of[:, None] == jnp.arange(slot_count)[None, :]) & routed[:, None]
    filled = jnp.any(hits, axis=0)
    source = jnp.sum(jnp.where(hits, order_ids[:, None], 0), axis=0) + jnp.where(
        filled, 0, row_count
    )
    slot_label = jnp.sum(jnp.where(hits, (local_group + 1)[:, None], 0), axis=0)

    def pack(vectors):
        padded = jnp.concatenate(
            [vectors, jnp.zeros((1,) + vectors.shape[1:], vectors.dtype)], axis=0
        )
        return jnp.take(padded, source, axis=0, mode="clip")

    def exchange(slots):
        shaped = slots.reshape((peer_count, capacity) + slots.shape[1:])
        moved = lax.all_to_all(shaped, "req", split_axis=0, concat_axis=0, tiled=True)
        return moved.reshape(slots.shape)

    def unpack(slots):
        taken = jnp.take(slots, slot_of, axis=0, mode="clip")
        return jnp.where(routed[:, None, None], taken, 0.0)

    def owner_apply(states, incoming, chosen):
        products = jnp.einsum("shj,ghij->gshi", incoming, states, precision=highest)
        total = jnp.where(chosen[0][:, None, None], products[0], 0.0)
        for group in range(1, group_count):
            total = total + jnp.where(chosen[group][:, None, None], products[group], 0.0)
        return total

    def cg_step(arrived, carry):
        solution, residual, direction, norm_now = carry
        shares = unpack(exchange(owner_apply(prompt_keys, arrived, chosen)))
        shared = weight_b * shares + own_matvec(own_keys, direction)
        product = (
            decay_b * shared
            + write_b * key_now * lane_sum(key_now * direction)
            + ridge_b * direction
        )
        step_size = norm_now / lane_sum(direction * product)
        solution = solution + step_size * direction
        residual = residual - step_size * product
        norm_next = lane_sum(residual * residual)
        direction = residual + norm_next / norm_now * direction
        return solution, residual, direction, norm_next

    label_row = jnp.broadcast_to(
        slot_label.astype(jnp.float32)[:, None, None], (slot_count, 1, head_size)
    )
    first = exchange(jnp.concatenate([pack(queries), label_row], axis=1))
    labels_in = first[:, head_count, 0]
    chosen = [labels_in == float(group + 1) for group in range(group_count)]
    carry = (
        jnp.zeros_like(queries),
        queries,
        queries,
        lane_sum(queries * queries),
    )
    carry = cg_step(first[:, :head_count], carry)
    carry = lax.fori_loop(
        1, ITERS - 1, lambda _, state: cg_step(exchange(pack(state[2])), state), carry
    )
    solution, residual, direction, norm_now = carry

    both = exchange(jnp.concatenate([pack(direction), pack(solution)], axis=1))
    held = both[:, :head_count]
    owner_out = jnp.concatenate(
        [
            owner_apply(prompt_keys, held, chosen),
            owner_apply(prompt_values, both[:, head_count:], chosen),
            owner_apply(prompt_values, held, chosen),
        ],
        axis=1,
    )
    returned = unpack(exchange(owner_out))
    own_out_partial = own_matvec(own_values, solution)
    own_out_direction = own_matvec(own_values, direction)
    partial = solution
    shares = returned[:, :head_count]
    shared = weight_col * shares + own_matvec(own_keys, direction)
    product = (
        decay_col * shared
        + write_col * key_now * jnp.sum(key_now * direction, axis=2, keepdims=True)
        + ridge_col * direction
    )
    step_last = norm_now[:, :, :1] / jnp.sum(direction * product, axis=2, keepdims=True)
    solution = partial + step_last * direction
    value_sum = returned[:, head_count : 2 * head_count] + step_last * returned[:, 2 * head_count :]
    own_out = own_out_partial + step_last * own_out_direction
    shared_out = weight_col * value_sum + own_out
    readout = decay_col * shared_out + write_col * value_now * jnp.sum(
        key_now * solution, axis=2, keepdims=True
    )
    normalized = (
        readout * lax.rsqrt(jnp.mean(readout * readout, axis=2, keepdims=True) + epsilon)
    ).astype(jnp.bfloat16)
    partial_value = jnp.dot(
        normalized.reshape(row_count, head_count * head_size),
        out_weight.reshape(head_count * head_size, model_width),
        preferred_element_type=jnp.float32,
    )
    head_peers = lax.axis_size("head")
    if head_peers == 2:
        me = lax.axis_index("head")
        width = model_width // 2
        mine = lax.dynamic_slice_in_dim(partial_value, me * width, width, axis=1)
        theirs = lax.dynamic_slice_in_dim(partial_value, (1 - me) * width, width, axis=1)
        attended = mine + lax.ppermute(theirs, "head", [(0, 1), (1, 0)])
    else:
        attended = lax.psum_scatter(
            partial_value.astype(jnp.bfloat16), "head", scatter_dimension=1, tiled=True
        ).astype(jnp.float32)
    widened_own = hidden.astype(jnp.float32)
    combined = jnp.where(mask_of_live[:, None], widened_own + attended, widened_own)
    return combined.astype(jnp.bfloat16)


def solution(mesh):
    in_specs = (
        P("req", "head"),
        P(),
        P(None, "head", None, None),
        P(None, "head", None, None),
        P("req", None, "head", None, None),
        P(None, None, "head"),
        P("req", "head"),
        P("head"),
        P("req", "head", None, None),
        P("req", "head", None, None),
        P("req", "head", None, None),
        P("req", "head", None, None),
        P("req"),
        P("req"),
        P("head", None, None),
    )
    out_specs = P("req", "head")
    return jax.shard_map(
        on_device, mesh=mesh, in_specs=in_specs, out_specs=out_specs, check_vma=False
    )
```

```python
import jax
import jax.numpy as jnp
from jax import lax
from jax.sharding import PartitionSpec as P

KW = 4
ITERS = 8
CAP = 6


epsilon = 1e-06
highest = lax.Precision.HIGHEST


def own_matvec(matrices, vectors):
    return jnp.sum(matrices * vectors[:, :, None, :], axis=3)


def on_device(
    hidden,
    norm_gain,
    qkv_weight,
    conv_weight,
    conv_state,
    gate_weight,
    prompt_weight,
    ridge_term,
    own_keys,
    own_values,
    prompt_keys,
    prompt_values,
    group_ids,
    lengths,
    out_weight,
):
    if lax.axis_size("head") == 2:
        other_half = lax.ppermute(hidden, "head", [(0, 1), (1, 0)])
        first_core = lax.axis_index("head") == 0
        gathered = jnp.where(
            first_core,
            jnp.concatenate([hidden, other_half], axis=1),
            jnp.concatenate([other_half, hidden], axis=1),
        )
    else:
        gathered = lax.all_gather(hidden, "head", axis=1, tiled=True)
    widened = gathered.astype(jnp.float32)
    scaled = (
        widened
        * lax.rsqrt(jnp.mean(widened * widened, axis=1, keepdims=True) + epsilon)
        * norm_gain
    )
    normed = scaled.astype(jnp.bfloat16)
    row_count, model_width = gathered.shape
    head_count = qkv_weight.shape[1]
    head_size = qkv_weight.shape[3]
    projected = jnp.dot(
        normed,
        qkv_weight.reshape(model_width, head_count * 3 * head_size),
        preferred_element_type=jnp.float32,
    ).reshape(row_count, head_count, 3, head_size)
    mixing = conv_weight[0] * projected
    for offset in range(1, KW):
        usable = (lengths >= offset).astype(jnp.float32)[:, None, None, None]
        mixing = (
            mixing + conv_weight[offset] * conv_state[:, offset - 1].astype(jnp.float32) * usable
        )
    active = jax.nn.silu(mixing)
    queries = active[:, :, 0]
    queries = queries * lax.rsqrt(jnp.sum(queries * queries, axis=2, keepdims=True) + epsilon)
    key_now = active[:, :, 1]
    key_now = key_now * lax.rsqrt(jnp.sum(key_now * key_now, axis=2, keepdims=True) + epsilon)
    value_now = active[:, :, 2]
    gate_logit = jnp.dot(
        normed, gate_weight.reshape(model_width, 2 * head_count), preferred_element_type=jnp.float32
    ).reshape(row_count, 2, head_count)
    decay_col = jax.nn.sigmoid(gate_logit[:, 0])[:, :, None]
    write_col = jax.nn.sigmoid(gate_logit[:, 1])[:, :, None]
    weight_col = prompt_weight[:, :, None]
    ridge_col = ridge_term[None, :, None]

    peer_count = lax.axis_size("req")
    group_count = prompt_keys.shape[0]
    capacity = CAP
    slot_count = peer_count * capacity
    mask_of_live = lengths > 0
    owner_of = group_ids // group_count
    local_group = group_ids % group_count
    order_ids = jnp.arange(row_count)
    earlier = (
        (order_ids[None, :] < order_ids[:, None])
        & (owner_of[None, :] == owner_of[:, None])
        & mask_of_live[None, :]
    )
    rank_of = jnp.sum(earlier.astype(jnp.int32), axis=1)
    routed = mask_of_live & (rank_of < capacity)
    slot_of = jnp.where(routed, owner_of * capacity + rank_of, 0)
    hits = (slot_of[:, None] == jnp.arange(slot_count)[None, :]) & routed[:, None]
    filled = jnp.any(hits, axis=0)
    source = jnp.sum(jnp.where(hits, order_ids[:, None], 0), axis=0) + jnp.where(
        filled, 0, row_count
    )
    slot_label = jnp.sum(jnp.where(hits, (local_group + 1)[:, None], 0), axis=0)

    def pack(vectors):
        padded = jnp.concatenate(
            [vectors, jnp.zeros((1,) + vectors.shape[1:], vectors.dtype)], axis=0
        )
        return jnp.take(padded, source, axis=0, mode="clip")

    def exchange(slots):
        shaped = slots.reshape((peer_count, capacity) + slots.shape[1:])
        moved = lax.all_to_all(shaped, "req", split_axis=0, concat_axis=0, tiled=True)
        return moved.reshape(slots.shape)

    def unpack(slots):
        taken = jnp.take(slots, slot_of, axis=0, mode="clip")
        return jnp.where(routed[:, None, None], taken, 0.0)

    def owner_apply(states, incoming, chosen):
        products = jnp.einsum("shj,ghij->gshi", incoming, states, precision=highest)
        total = jnp.where(chosen[0][:, None, None], products[0], 0.0)
        for group in range(1, group_count):
            total = total + jnp.where(chosen[group][:, None, None], products[group], 0.0)
        return total

    def cg_step(arrived, carry):
        solution, residual, direction, norm_now = carry
        shares = unpack(exchange(owner_apply(prompt_keys, arrived, chosen)))
        shared = weight_col * shares + own_matvec(own_keys, direction)
        product = (
            decay_col * shared
            + write_col * key_now * jnp.sum(key_now * direction, axis=2, keepdims=True)
            + ridge_col * direction
        )
        step_size = norm_now / jnp.sum(direction * product, axis=2, keepdims=True)
        solution = solution + step_size * direction
        residual = residual - step_size * product
        norm_next = jnp.sum(residual * residual, axis=2, keepdims=True)
        direction = residual + norm_next / norm_now * direction
        return solution, residual, direction, norm_next

    label_row = jnp.broadcast_to(
        slot_label.astype(jnp.float32)[:, None, None], (slot_count, 1, head_size)
    )
    first = exchange(jnp.concatenate([pack(queries), label_row], axis=1))
    labels_in = first[:, head_count, 0]
    chosen = [labels_in == float(group + 1) for group in range(group_count)]
    carry = (
        jnp.zeros_like(queries),
        queries,
        queries,
        jnp.sum(queries * queries, axis=2, keepdims=True),
    )
    carry = cg_step(first[:, :head_count], carry)
    carry = lax.fori_loop(
        1, ITERS - 1, lambda _, state: cg_step(exchange(pack(state[2])), state), carry
    )
    solution, residual, direction, norm_now = carry

    both = exchange(jnp.concatenate([pack(direction), pack(solution)], axis=1))
    held = both[:, :head_count]
    owner_out = jnp.concatenate(
        [
            owner_apply(prompt_keys, held, chosen),
            owner_apply(prompt_values, both[:, head_count:], chosen),
            owner_apply(prompt_values, held, chosen),
        ],
        axis=1,
    )
    returned = unpack(exchange(owner_out))
    own_out_partial = own_matvec(own_values, solution)
    own_out_direction = own_matvec(own_values, direction)
    partial = solution
    shares = returned[:, :head_count]
    shared = weight_col * shares + own_matvec(own_keys, direction)
    product = (
        decay_col * shared
        + write_col * key_now * jnp.sum(key_now * direction, axis=2, keepdims=True)
        + ridge_col * direction
    )
    step_last = norm_now / jnp.sum(direction * product, axis=2, keepdims=True)
    solution = partial + step_last * direction
    value_sum = returned[:, head_count : 2 * head_count] + step_last * returned[:, 2 * head_count :]
    own_out = own_out_partial + step_last * own_out_direction
    shared_out = weight_col * value_sum + own_out
    readout = decay_col * shared_out + write_col * value_now * jnp.sum(
        key_now * solution, axis=2, keepdims=True
    )
    normalized = (
        readout * lax.rsqrt(jnp.mean(readout * readout, axis=2, keepdims=True) + epsilon)
    ).astype(jnp.bfloat16)
    flat = normalized.reshape(row_count, head_count * head_size)
    weight_flat = out_weight.reshape(head_count * head_size, model_width)
    head_peers = lax.axis_size("head")
    if head_peers == 2:
        me = lax.axis_index("head")
        width = model_width // 2
        theirs = jnp.dot(
            flat,
            lax.dynamic_slice_in_dim(weight_flat, (1 - me) * width, width, axis=1),
            preferred_element_type=jnp.float32,
        )
        arriving = lax.ppermute(theirs, "head", [(0, 1), (1, 0)])
        mine = jnp.dot(
            flat,
            lax.dynamic_slice_in_dim(weight_flat, me * width, width, axis=1),
            preferred_element_type=jnp.float32,
        )
        attended = mine + arriving
    else:
        partial_value = jnp.dot(flat, weight_flat, preferred_element_type=jnp.float32)
        attended = lax.psum_scatter(
            partial_value.astype(jnp.bfloat16), "head", scatter_dimension=1, tiled=True
        ).astype(jnp.float32)
    widened_own = hidden.astype(jnp.float32)
    combined = jnp.where(mask_of_live[:, None], widened_own + attended, widened_own)
    return combined.astype(jnp.bfloat16)


def solution(mesh):
    in_specs = (
        P("req", "head"),
        P(),
        P(None, "head", None, None),
        P(None, "head", None, None),
        P("req", None, "head", None, None),
        P(None, None, "head"),
        P("req", "head"),
        P("head"),
        P("req", "head", None, None),
        P("req", "head", None, None),
        P("req", "head", None, None),
        P("req", "head", None, None),
        P("req"),
        P("req"),
        P("head", None, None),
    )
    out_specs = P("req", "head")
    return jax.shard_map(
        on_device, mesh=mesh, in_specs=in_specs, out_specs=out_specs, check_vma=False
    )
```

```python
import jax
import jax.numpy as jnp
from jax import lax
from jax.sharding import PartitionSpec as P

KW = 4
ITERS = 8
CAP = 6


epsilon = 1e-06
highest = lax.Precision.HIGHEST


def own_matvec(matrices, vectors):
    return jnp.sum(matrices * vectors[:, :, None, :], axis=3)


def on_device(
    hidden,
    norm_gain,
    qkv_weight,
    conv_weight,
    conv_state,
    gate_weight,
    prompt_weight,
    ridge_term,
    own_keys,
    own_values,
    prompt_keys,
    prompt_values,
    group_ids,
    lengths,
    out_weight,
):
    if lax.axis_size("head") == 2:
        other_half = lax.ppermute(hidden, "head", [(0, 1), (1, 0)])
        first_core = lax.axis_index("head") == 0
        gathered = jnp.where(
            first_core,
            jnp.concatenate([hidden, other_half], axis=1),
            jnp.concatenate([other_half, hidden], axis=1),
        )
    else:
        gathered = lax.all_gather(hidden, "head", axis=1, tiled=True)
    widened = gathered.astype(jnp.float32)
    scaled = (
        widened
        * lax.rsqrt(jnp.mean(widened * widened, axis=1, keepdims=True) + epsilon)
        * norm_gain
    )
    normed = scaled.astype(jnp.bfloat16)
    row_count, model_width = gathered.shape
    head_count = qkv_weight.shape[1]
    head_size = qkv_weight.shape[3]
    projected = jnp.dot(
        normed,
        qkv_weight.reshape(model_width, head_count * 3 * head_size),
        preferred_element_type=jnp.float32,
    ).reshape(row_count, head_count, 3, head_size)
    mixing = conv_weight[0] * projected
    for offset in range(1, KW):
        usable = (lengths >= offset).astype(jnp.float32)[:, None, None, None]
        mixing = (
            mixing + conv_weight[offset] * conv_state[:, offset - 1].astype(jnp.float32) * usable
        )
    active = jax.nn.silu(mixing)
    queries = active[:, :, 0]
    queries = queries * lax.rsqrt(jnp.sum(queries * queries, axis=2, keepdims=True) + epsilon)
    key_now = active[:, :, 1]
    key_now = key_now * lax.rsqrt(jnp.sum(key_now * key_now, axis=2, keepdims=True) + epsilon)
    value_now = active[:, :, 2]
    gate_logit = jnp.dot(
        normed, gate_weight.reshape(model_width, 2 * head_count), preferred_element_type=jnp.float32
    ).reshape(row_count, 2, head_count)
    decay_col = jax.nn.sigmoid(gate_logit[:, 0])[:, :, None]
    write_col = jax.nn.sigmoid(gate_logit[:, 1])[:, :, None]
    weight_col = prompt_weight[:, :, None]
    ridge_col = ridge_term[None, :, None]

    peer_count = lax.axis_size("req")
    group_count = prompt_keys.shape[0]
    capacity = CAP
    slot_count = peer_count * capacity
    mask_of_live = lengths > 0
    owner_of = group_ids // group_count
    local_group = group_ids % group_count
    order_ids = jnp.arange(row_count)
    earlier = (
        (order_ids[None, :] < order_ids[:, None])
        & (owner_of[None, :] == owner_of[:, None])
        & mask_of_live[None, :]
    )
    rank_of = jnp.sum(earlier.astype(jnp.int32), axis=1)
    routed = mask_of_live & (rank_of < capacity)
    slot_of = jnp.where(routed, owner_of * capacity + rank_of, 0)
    hits = (slot_of[:, None] == jnp.arange(slot_count)[None, :]) & routed[:, None]
    filled = jnp.any(hits, axis=0)
    source = jnp.sum(jnp.where(hits, order_ids[:, None], 0), axis=0) + jnp.where(
        filled, 0, row_count
    )
    slot_label = jnp.sum(jnp.where(hits, (local_group + 1)[:, None], 0), axis=0)

    def pack(vectors):
        padded = jnp.concatenate(
            [vectors, jnp.zeros((1,) + vectors.shape[1:], vectors.dtype)], axis=0
        )
        return jnp.take(padded, source, axis=0, mode="clip")

    def exchange(slots):
        shaped = slots.reshape((peer_count, capacity) + slots.shape[1:])
        moved = lax.all_to_all(shaped, "req", split_axis=0, concat_axis=0, tiled=True)
        return moved.reshape(slots.shape)

    def unpack(slots):
        taken = jnp.take(slots, slot_of, axis=0, mode="clip")
        return jnp.where(routed[:, None, None], taken, 0.0)

    def owner_apply(states, incoming, chosen):
        split = jnp.stack(
            [jnp.where(chosen[group][:, None, None], incoming, 0.0) for group in range(group_count)]
        )
        return jnp.einsum("gshj,ghij->shi", split, states, precision=highest)

    def cg_step(arrived, carry):
        solution, residual, direction, norm_now = carry
        shares = unpack(exchange(owner_apply(prompt_keys, arrived, chosen)))
        shared = weight_col * shares + own_matvec(own_keys, direction)
        product = (
            decay_col * shared
            + write_col * key_now * jnp.sum(key_now * direction, axis=2, keepdims=True)
            + ridge_col * direction
        )
        step_size = norm_now / jnp.sum(direction * product, axis=2, keepdims=True)
        solution = solution + step_size * direction
        residual = residual - step_size * product
        norm_next = jnp.sum(residual * residual, axis=2, keepdims=True)
        direction = residual + norm_next / norm_now * direction
        return solution, residual, direction, norm_next

    label_row = jnp.broadcast_to(
        slot_label.astype(jnp.float32)[:, None, None], (slot_count, 1, head_size)
    )
    first = exchange(jnp.concatenate([pack(queries), label_row], axis=1))
    labels_in = first[:, head_count, 0]
    chosen = [labels_in == float(group + 1) for group in range(group_count)]
    carry = (
        jnp.zeros_like(queries),
        queries,
        queries,
        jnp.sum(queries * queries, axis=2, keepdims=True),
    )
    carry = cg_step(first[:, :head_count], carry)
    carry = lax.fori_loop(
        1, ITERS - 1, lambda _, state: cg_step(exchange(pack(state[2])), state), carry
    )
    solution, residual, direction, norm_now = carry

    both = exchange(jnp.concatenate([pack(direction), pack(solution)], axis=1))
    held = both[:, :head_count]
    owner_out = jnp.concatenate(
        [
            owner_apply(prompt_keys, held, chosen),
            owner_apply(prompt_values, both[:, head_count:], chosen),
            owner_apply(prompt_values, held, chosen),
        ],
        axis=1,
    )
    returned = unpack(exchange(owner_out))
    own_out_partial = own_matvec(own_values, solution)
    own_out_direction = own_matvec(own_values, direction)
    partial = solution
    shares = returned[:, :head_count]
    shared = weight_col * shares + own_matvec(own_keys, direction)
    product = (
        decay_col * shared
        + write_col * key_now * jnp.sum(key_now * direction, axis=2, keepdims=True)
        + ridge_col * direction
    )
    step_last = norm_now / jnp.sum(direction * product, axis=2, keepdims=True)
    solution = partial + step_last * direction
    value_sum = returned[:, head_count : 2 * head_count] + step_last * returned[:, 2 * head_count :]
    own_out = own_out_partial + step_last * own_out_direction
    shared_out = weight_col * value_sum + own_out
    readout = decay_col * shared_out + write_col * value_now * jnp.sum(
        key_now * solution, axis=2, keepdims=True
    )
    normalized = (
        readout * lax.rsqrt(jnp.mean(readout * readout, axis=2, keepdims=True) + epsilon)
    ).astype(jnp.bfloat16)
    partial_value = jnp.dot(
        normalized.reshape(row_count, head_count * head_size),
        out_weight.reshape(head_count * head_size, model_width),
        preferred_element_type=jnp.float32,
    )
    head_peers = lax.axis_size("head")
    if head_peers == 2:
        me = lax.axis_index("head")
        width = model_width // 2
        mine = lax.dynamic_slice_in_dim(partial_value, me * width, width, axis=1)
        theirs = lax.dynamic_slice_in_dim(partial_value, (1 - me) * width, width, axis=1)
        attended = mine + lax.ppermute(theirs, "head", [(0, 1), (1, 0)])
    else:
        attended = lax.psum_scatter(
            partial_value.astype(jnp.bfloat16), "head", scatter_dimension=1, tiled=True
        ).astype(jnp.float32)
    widened_own = hidden.astype(jnp.float32)
    combined = jnp.where(mask_of_live[:, None], widened_own + attended, widened_own)
    return combined.astype(jnp.bfloat16)


def solution(mesh):
    in_specs = (
        P("req", "head"),
        P(),
        P(None, "head", None, None),
        P(None, "head", None, None),
        P("req", None, "head", None, None),
        P(None, None, "head"),
        P("req", "head"),
        P("head"),
        P("req", "head", None, None),
        P("req", "head", None, None),
        P("req", "head", None, None),
        P("req", "head", None, None),
        P("req"),
        P("req"),
        P("head", None, None),
    )
    out_specs = P("req", "head")
    return jax.shard_map(
        on_device, mesh=mesh, in_specs=in_specs, out_specs=out_specs, check_vma=False
    )
```
